512 devices in a mesh: seq: 32 (over z, core), head: 16 (over y, x).
Axes of the slice: x: 4, y: 4, z: 16, core: 2. Of those that a mesh axis runs over, the one named last changes fastest.
Arguments:
- head_inputs: float32 [16384, 8192], P('seq', 'head'), may hold values from -0.625 to 0.625
- input_proj: float32 [16384, 128], P('seq'), may hold values from -1.75 to 1.75
- output_mapping: float32 [16384, 128], P('seq'), may hold values from -1.75 to 1.75
- decay_codes: int32 [128, 16384], P('head', 'seq'), may hold values from 0 to 15
- boundary: int32 [16384], P('seq'), may hold values 0 or 1
- head_decay_speeds: float32 [128], P('head'), may hold values from 0 to 1, as said below
- out_grad: float32 [16384, 8192], P('seq', 'head'), may hold values from -0.0625 to 0.0625
Outputs:
- grad_inputs: float32 [16384, 8192], P('seq', 'head')
- grad_in_proj: float32 [16384, 128], P(('seq', 'head'))
- grad_out_proj: float32 [16384, 128], P(('seq', 'head'))
The draws below stay inside these ranges and needn't reach their ends.
Inputs may be any that keep to these rules, and one draw needn't show every extreme that they name: `head_decay_speeds`: each head's decay rate is positive.
All inputs are finite; a program needn't handle non-finite values. No bound on the sum of `boundary` on one device may be relied on, other than what follows from the above.
Results may differ from the reference program's by a relative error of at most 0.0001.
Values sent between devices are 32-bit elements; how exact they have to be, the bound alone decides.
No kernel may reach another device: no remote copies, remote signals or barrier semaphores. Data moves between devices by JAX's collectives and lax.ppermute only.
A program may use at most 64 MiB of HBM per device.

```python
import jax
import jax.numpy as jnp
from jax import lax

HEADS = 128
HEAD_DIM = 64
STATE = 128
TOK_DEV = 512
TOKENS = 16384
N_SEQ = 32


def draw_head_decay_speeds(key, part):
    key_pick, key_slow, key_fast = jax.random.split(key, 3)
    picker = jax.random.uniform(key_pick, (HEADS,), jnp.float32)
    fast_share = 0.5
    slow_rate = jnp.exp(jax.random.uniform(key_slow, (HEADS,), jnp.float32, jnp.log(0.05), jnp.log(0.6))) / TOKENS
    fast_rate = jnp.exp(jax.random.uniform(key_fast, (HEADS,), jnp.float32, jnp.log(1.0 / 40.0), jnp.log(1.0 / 25.0)))
    return jnp.where(picker < fast_share, fast_rate, slow_rate).astype(jnp.float32)


def touch_ends(drawn, key, least, top_value):
    index_at = [jax.random.randint(jax.random.fold_in(key, axis), (), 0, length) for axis, length in enumerate(drawn.shape)]
    main_axis = drawn.shape.index(max(drawn.shape))
    beside = index_at[:main_axis] + [(index_at[main_axis] + 1) % drawn.shape[main_axis]] + index_at[main_axis + 1:]
    return drawn.at[tuple(index_at)].set(least).at[tuple(beside)].set(top_value)


def block_scale(own_key, dims, cuts, smallest, largest):
    def one(position, shards_of):
        heights = jax.random.uniform(jax.random.fold_in(jax.random.fold_in(own_key, 6), position), (shards_of,), jnp.float32, smallest / len(cuts), largest / len(cuts))
        return jnp.repeat(jnp.exp(heights), dims[position] // shards_of).reshape((-1,) + (1,) * (len(dims) - position - 1))

    factor_of = one(*cuts[0])
    for cut in cuts[1:]:
        factor_of = factor_of * one(*cut)
    return factor_of


def scatter_about(own_key, extent, deviation, most, shards=(), kind=jnp.bfloat16):
    array = deviation * jax.random.normal(own_key, extent, jnp.float32)
    if shards:
        array = array * block_scale(own_key, extent, shards, -0.22, 0.18)
    return jnp.clip(array, -most, most).astype(kind)


def setup_inputs(seed: int = 0) -> dict:
    key_of = jax.random.split(jax.random.key(seed), 8)
    head_inputs = scatter_about(key_of[0], (TOKENS, HEADS * HEAD_DIM), 0.1, 0.625, ((0, 32), (1, 16)), jnp.float32)
    input_proj = scatter_about(key_of[1], (TOKENS, STATE), 0.3, 1.75, ((0, 32),), jnp.float32)
    output_mapping = scatter_about(key_of[2], (TOKENS, STATE), 0.3, 1.75, ((0, 32),), jnp.float32)
    decay_codes = touch_ends(jax.random.randint(key_of[3], (HEADS, TOKENS), 0, 16), jax.random.fold_in(key_of[3], 1), 0, 15).astype(jnp.int32)
    boundary = touch_ends((jax.random.randint(key_of[4], (TOKENS,), 0, 4096) < 1).astype(jnp.int32), jax.random.fold_in(key_of[4], 1), 0, 1)
    head_decay_speeds = draw_head_decay_speeds(jax.random.fold_in(key_of[7], 71), 0)
    out_grad = scatter_about(key_of[6], (TOKENS, HEADS * HEAD_DIM), 0.01, 0.0625, ((0, 32), (1, 16)), jnp.float32)
    return {"head_inputs": head_inputs, "input_proj": input_proj, "output_mapping": output_mapping, "decay_codes": decay_codes, "boundary": boundary, "head_decay_speeds": head_decay_speeds, "out_grad": out_grad}


sudden_falloff = 0.35
highest = lax.Precision.HIGHEST

def increment_values():
    levels = jnp.arange(16, dtype=jnp.int32)
    return 0.5 * 4.0 ** (levels.astype(jnp.float32) / 15.0)

def block_step(state, pieces):
    scaled_blk, in_blk, out_blk, decay_blk = pieces
    cumul = jnp.cumsum(decay_blk, axis=1)
    group_total = cumul[:, -1]
    positions = jnp.arange(TOK_DEV, dtype=jnp.int32)
    lower_mask = positions[:, None] >= positions[None, :]
    decay_gap = jnp.where(lower_mask[None], cumul[:, :, None] - cumul[:, None, :], 0.0)
    decay_mat = jnp.where(lower_mask[None], jnp.exp(decay_gap), 0.0)
    scores = jnp.dot(out_blk, in_blk.T, precision=highest)
    inner = jnp.einsum('hts,shp->thp', scores[None] * decay_mat, scaled_blk, precision=highest)
    carried = jnp.einsum('tn,hpn->thp', out_blk, state, precision=highest) * jnp.exp(cumul).T[:, :, None]
    weights = jnp.exp(group_total[:, None] - cumul).T[:, :, None]
    new_state = jnp.exp(group_total)[:, None, None] * state + jnp.einsum('shp,sn->hpn', scaled_blk * weights, in_blk, precision=highest)
    return (new_state, (inner + carried).reshape(TOK_DEV, HEADS * HEAD_DIM))

def reference(head_inputs, input_proj, output_mapping, decay_codes, boundary, head_decay_speeds, out_grad):
    increment_length = increment_values()[decay_codes]
    logarithm_decay = -head_decay_speeds[:, None] * increment_length - sudden_falloff * boundary.astype(jnp.float32)[None, :]

    def forward(inputs_all, in_all, out_all):
        scaled = inputs_all.reshape(TOKENS, HEADS, HEAD_DIM) * increment_length.T[:, :, None]
        scaled_blocks = scaled.reshape(N_SEQ, TOK_DEV, HEADS, HEAD_DIM)
        in_blocks = in_all.reshape(N_SEQ, TOK_DEV, STATE)
        out_blocks = out_all.reshape(N_SEQ, TOK_DEV, STATE)
        decay_blocks = logarithm_decay.reshape(HEADS, N_SEQ, TOK_DEV).transpose(1, 0, 2)
        initial = jnp.zeros((HEADS, HEAD_DIM, STATE), jnp.float32)
        final_state, outputs = lax.scan(jax.checkpoint(block_step), initial, (scaled_blocks, in_blocks, out_blocks, decay_blocks))
        return outputs.reshape(TOKENS, HEADS * HEAD_DIM)
    outputs, vector_jacobian = jax.vjp(forward, head_inputs, input_proj, output_mapping)
    grad_inputs, grad_in_proj, grad_out_proj = vector_jacobian(out_grad)
    return (grad_inputs, grad_in_proj, grad_out_proj)
```

```python
import jax
import jax.numpy as jnp
from jax import lax
from jax.experimental import pallas as pl
from jax.experimental.pallas import tpu as pltpu
from jax.sharding import PartitionSpec as P

sudden_falloff = 0.35
highest = lax.Precision.HIGHEST
HEADS_PER_STEP = 2


def step_table(decay_codes):
    levels = jnp.arange(16, dtype=jnp.int32)
    values = 0.5 * 4.0 ** (levels.astype(jnp.float32) / 15.0)
    matching_label = decay_codes[None, :, :] == levels[:, None, None]
    return jnp.sum(jnp.where(matching_label, values[:, None, None], 0.0), axis=0)


def spread_heads(per_head, head_width):
    head_count, tok_count = per_head.shape
    wide = jnp.broadcast_to(per_head.T[:, :, None], (tok_count, head_count, head_width))
    return wide.reshape(tok_count, head_count * head_width)


def block_kernel(cum_row_ref, cum_col_ref, scores_t_ref, in_ref, grad_ref, flow_ref, acc_ref):
    step = pl.program_id(0)

    @pl.when(step == 0)
    def _():
        acc_ref[...] = jnp.zeros_like(acc_ref)

    tok = scores_t_ref.shape[0]
    width = in_ref.shape[1] // HEADS_PER_STEP
    rows = lax.broadcasted_iota(jnp.int32, (tok, tok), 0)
    cols = lax.broadcasted_iota(jnp.int32, (tok, tok), 1)
    later = cols >= rows
    scores_t = scores_t_ref[...]
    for k in range(HEADS_PER_STEP):
        gap = cum_row_ref[k] - cum_col_ref[k]
        decay_t = jnp.where(later, jnp.exp(jnp.where(later, gap, 0.0)), 0.0)
        own_in = in_ref[:, k * width:(k + 1) * width]
        own_grad = grad_ref[:, k * width:(k + 1) * width]
        flow_ref[:, k * width:(k + 1) * width] = jnp.dot(
            scores_t * decay_t, own_grad, precision=highest, preferred_element_type=jnp.float32
        )
        pair_t = lax.dot_general(
            own_in, own_grad, (((1,), (1,)), ((), ())), precision=highest,
            preferred_element_type=jnp.float32,
        )
        acc_ref[...] += pair_t * decay_t


def block_terms(cumul, scores_t, scaled_in, out_grad):
    head_count, tok = cumul.shape
    chan = scaled_in.shape[1]
    lanes = chan // head_count * HEADS_PER_STEP
    cum_row = cumul.reshape(head_count, 1, tok)
    cum_col = cumul.reshape(head_count, tok, 1)
    return pl.pallas_call(
        block_kernel,
        grid=(head_count // HEADS_PER_STEP,),
        in_specs=[
            pl.BlockSpec((HEADS_PER_STEP, 1, tok), lambda j: (j, 0, 0)),
            pl.BlockSpec((HEADS_PER_STEP, tok, 1), lambda j: (j, 0, 0)),
            pl.BlockSpec((tok, tok), lambda j: (0, 0)),
            pl.BlockSpec((tok, lanes), lambda j: (0, j)),
            pl.BlockSpec((tok, lanes), lambda j: (0, j)),
        ],
        out_specs=[
            pl.BlockSpec((tok, lanes), lambda j: (0, j)),
            pl.BlockSpec((tok, tok), lambda j: (0, 0)),
        ],
        out_shape=[
            jax.ShapeDtypeStruct((tok, chan), jnp.float32),
            jax.ShapeDtypeStruct((tok, tok), jnp.float32),
        ],
    )(cum_row, cum_col, scores_t, scaled_in, out_grad)


def pack(state, total):
    head_count, width, state_width = state.shape
    tot_rows = jnp.zeros((8, state_width), jnp.float32)
    tot_rows = lax.dynamic_update_slice(
        tot_rows, jnp.broadcast_to(total[:, None], (head_count, state_width)), (0, 0)
    )
    return jnp.concatenate([state.reshape(head_count * width, state_width), tot_rows], axis=0)


def join(earlier, later, head_count, width):
    rows = head_count * width
    later_tot = later[rows:rows + head_count, 0]
    scale = jnp.concatenate(
        [jnp.repeat(jnp.exp(later_tot), width), jnp.ones((8,), jnp.float32)]
    )
    return scale[:, None] * earlier + later


def chip_scan(state, total, backward):
    count = lax.axis_size("seq")
    index = lax.axis_index("seq")
    head_count, width, state_width = state.shape
    half = head_count // 2
    position = count - 1 - index if backward else index
    sub = position % 2

    def move(value, delta):
        if backward:
            pairs = [(i, i - delta) for i in range(delta, count)]
        else:
            pairs = [(i, i + delta) for i in range(count - delta)]
        return lax.ppermute(value, "seq", pairs)

    def heads(lo):
        return pack(
            lax.dynamic_slice_in_dim(state, lo, half, 0),
            lax.dynamic_slice_in_dim(total, lo, half, 0),
        )

    swap = [(i, i ^ 1) for i in range(count)]
    own_half = heads(sub * half)
    other_half = heads((1 - sub) * half)
    got = lax.ppermute(other_half, "seq", swap)
    first = jnp.where(sub == 0, own_half, got)
    second = jnp.where(sub == 0, got, own_half)
    chip_total = join(first, second, half, width)
    running = move(chip_total, 2)
    distance = 1
    while 2 * distance < count:
        running = join(move(running, 2 * distance), running, half, width)
        distance *= 2
    after_first = join(running, first, half, width)
    outgoing = jnp.where(sub == 0, after_first, running)
    incoming = lax.ppermute(outgoing, "seq", swap)
    mine = jnp.where(sub == 0, running, after_first)
    low = jnp.where(sub == 0, mine, incoming)
    high = jnp.where(sub == 0, incoming, mine)
    rows = half * width
    return jnp.concatenate([low[:rows], high[:rows]], axis=0).reshape(
        head_count, width, state_width
    )


def per_device(
    head_inputs, input_proj, output_mapping, decay_codes, boundary, head_decay_speeds, out_grad
):
    tok_count = head_inputs.shape[0]
    head_count = decay_codes.shape[0]
    head_width = head_inputs.shape[1] // head_count
    state_width = input_proj.shape[1]
    increment_length = step_table(decay_codes)
    logarithm_decay = (
        -head_decay_speeds[:, None] * increment_length
        - sudden_falloff * boundary.astype(jnp.float32)[None, :]
    )
    cumul = jnp.cumsum(logarithm_decay, axis=1)
    group_total = cumul[:, -1]
    to_end = spread_heads(jnp.exp(group_total[:, None] - cumul), head_width)
    from_start = spread_heads(jnp.exp(cumul), head_width)
    scaled_in = head_inputs * spread_heads(increment_length, head_width)
    weighted_in = scaled_in * to_end
    weighted_grad = out_grad * from_start
    ends = jnp.einsum("tk,tn->kn", weighted_in, input_proj, precision=highest)
    starts = jnp.einsum("tk,tn->kn", weighted_grad, output_mapping, precision=highest)
    state_in = chip_scan(
        ends.reshape(head_count, head_width, state_width), group_total, False
    )
    state_grad = chip_scan(
        starts.reshape(head_count, head_width, state_width), group_total, True
    )

    scores_t = jnp.einsum("sn,tn->st", input_proj, output_mapping, precision=highest)
    grad_scaled, grad_scores_t = block_terms(cumul, scores_t, scaled_in, out_grad)
    block_b = jnp.dot(grad_scores_t, output_mapping, precision=highest)
    block_c = jnp.einsum("st,sn->tn", grad_scores_t, input_proj, precision=highest)

    flat_in = state_in.reshape(head_count * head_width, state_width)
    flat_grad = state_grad.reshape(head_count * head_width, state_width)
    carry_c = jnp.dot(weighted_grad, flat_in, precision=highest)
    carry_b = jnp.dot(weighted_in, flat_grad, precision=highest)
    carry_x = to_end * jnp.einsum("tn,kn->tk", input_proj, flat_grad, precision=highest)
    grad_inputs = (grad_scaled + carry_x) * spread_heads(increment_length, head_width)

    both = jnp.concatenate([block_b + carry_b, block_c + carry_c], axis=1)
    parts = lax.axis_size("head")
    spread = lax.all_to_all(both, "head", 0, 0, tiled=True)
    summed = spread.reshape(parts, tok_count // parts, 2 * state_width).sum(axis=0)
    return (grad_inputs, summed[:, :state_width], summed[:, state_width:])


def solution(mesh):
    return jax.shard_map(
        per_device,
        mesh=mesh,
        in_specs=(
            P("seq", "head"),
            P("seq", None),
            P("seq", None),
            P("head", "seq"),
            P("seq"),
            P("head"),
            P("seq", "head"),
        ),
        out_specs=(P("seq", "head"), P(("seq", "head"), None), P(("seq", "head"), None)),
        check_vma=False,
    )
```

```python
import jax
import jax.numpy as jnp
from jax import lax
from jax.experimental import pallas as pl
from jax.experimental.pallas import tpu as pltpu
from jax.sharding import PartitionSpec as P

sudden_falloff = 0.35
highest = lax.Precision.HIGHEST
HEADS_PER_STEP = 2


def step_table(decay_codes):
    levels = jnp.arange(16, dtype=jnp.int32)
    values = 0.5 * 4.0 ** (levels.astype(jnp.float32) / 15.0)
    matching_label = decay_codes[None, :, :] == levels[:, None, None]
    return jnp.sum(jnp.where(matching_label, values[:, None, None], 0.0), axis=0)


def spread_heads(per_head, head_width):
    head_count, tok_count = per_head.shape
    wide = jnp.broadcast_to(per_head.T[:, :, None], (tok_count, head_count, head_width))
    return wide.reshape(tok_count, head_count * head_width)


def block_kernel(cum_row_ref, cum_col_ref, scores_t_ref, in_ref, grad_ref, flow_ref, acc_ref):
    step = pl.program_id(0)

    @pl.when(step == 0)
    def _():
        acc_ref[...] = jnp.zeros_like(acc_ref)

    tok = scores_t_ref.shape[0]
    width = in_ref.shape[1] // HEADS_PER_STEP
    rows = lax.broadcasted_iota(jnp.int32, (tok, tok), 0)
    cols = lax.broadcasted_iota(jnp.int32, (tok, tok), 1)
    later = cols >= rows
    scores_t = scores_t_ref[...]
    for k in range(HEADS_PER_STEP):
        gap = cum_row_ref[k] - cum_col_ref[k]
        decay_t = jnp.where(later, jnp.exp(jnp.where(later, gap, 0.0)), 0.0)
        own_in = in_ref[:, k * width:(k + 1) * width]
        own_grad = grad_ref[:, k * width:(k + 1) * width]
        flow_ref[:, k * width:(k + 1) * width] = jnp.dot(
            scores_t * decay_t, own_grad, precision=highest, preferred_element_type=jnp.float32
        )
        pair_t = lax.dot_general(
            own_in, own_grad, (((1,), (1,)), ((), ())), precision=highest,
            preferred_element_type=jnp.float32,
        )
        acc_ref[...] += pair_t * decay_t


def block_terms(cumul, scores_t, scaled_in, out_grad):
    head_count, tok = cumul.shape
    chan = scaled_in.shape[1]
    lanes = chan // head_count * HEADS_PER_STEP
    cum_row = cumul.reshape(head_count, 1, tok)
    cum_col = cumul.reshape(head_count, tok, 1)
    return pl.pallas_call(
        block_kernel,
        grid=(head_count // HEADS_PER_STEP,),
        in_specs=[
            pl.BlockSpec((HEADS_PER_STEP, 1, tok), lambda j: (j, 0, 0)),
            pl.BlockSpec((HEADS_PER_STEP, tok, 1), lambda j: (j, 0, 0)),
            pl.BlockSpec((tok, tok), lambda j: (0, 0)),
            pl.BlockSpec((tok, lanes), lambda j: (0, j)),
            pl.BlockSpec((tok, lanes), lambda j: (0, j)),
        ],
        out_specs=[
            pl.BlockSpec((tok, lanes), lambda j: (0, j)),
            pl.BlockSpec((tok, tok), lambda j: (0, 0)),
        ],
        out_shape=[
            jax.ShapeDtypeStruct((tok, chan), jnp.float32),
            jax.ShapeDtypeStruct((tok, tok), jnp.float32),
        ],
    )(cum_row, cum_col, scores_t, scaled_in, out_grad)


def pack_total(total, state_width):
    head_count = total.shape[0]
    rows = jnp.zeros((8, state_width), jnp.float32)
    return lax.dynamic_update_slice(
        rows, jnp.broadcast_to(total[:, None], (head_count, state_width)), (0, 0)
    )


def join(earlier, later, later_total):
    return jnp.exp(later_total)[:, None, None] * earlier + later


def pick(flag, when_true, when_false):
    return jnp.where(flag, when_true, when_false)


def chip_scans(ends, starts, total):
    chips = lax.axis_size("z")
    chip = lax.axis_index("z")
    core = lax.axis_index("core")
    head_count, width, state_width = ends.shape
    half = head_count // 2
    rows = half * width
    swap = [(0, 1), (1, 0)]
    mine_lo = core * half
    other_lo = (1 - core) * half

    def heads(value, lo):
        return lax.dynamic_slice_in_dim(value, lo, half, 0)

    own_x, own_y, own_t = heads(ends, mine_lo), heads(starts, mine_lo), heads(total, mine_lo)
    outgoing = jnp.concatenate(
        [
            heads(ends, other_lo).reshape(rows, state_width),
            heads(starts, other_lo).reshape(rows, state_width),
            pack_total(heads(total, other_lo), state_width),
        ],
        axis=0,
    )
    incoming = lax.ppermute(outgoing, "core", swap)
    got_x = incoming[:rows].reshape(half, width, state_width)
    got_y = incoming[rows:2 * rows].reshape(half, width, state_width)
    got_t = incoming[2 * rows:2 * rows + half, 0]
    is_first = core == 0
    x_first, x_second = pick(is_first, own_x, got_x), pick(is_first, got_x, own_x)
    y_first, y_second = pick(is_first, own_y, got_y), pick(is_first, got_y, own_y)
    t_first, t_second = pick(is_first, own_t, got_t), pick(is_first, got_t, own_t)
    chip_x = join(x_first, x_second, t_second)
    chip_y = join(y_second, y_first, t_first)
    chip_t = t_first + t_second
    gathered = lax.all_gather(
        jnp.concatenate(
            [
                chip_x.reshape(rows, state_width),
                chip_y.reshape(rows, state_width),
                pack_total(chip_t, state_width),
            ],
            axis=0,
        ),
        "z",
    )
    all_x = gathered[:, :rows].reshape(chips, half, width, state_width)
    all_y = gathered[:, rows:2 * rows].reshape(chips, half, width, state_width)
    all_t = gathered[:, 2 * rows:2 * rows + half, 0]
    src = jnp.arange(chips, dtype=jnp.int32)
    between_fwd = (src[:, None] < src[None, :]) & (src[None, :] < chip)
    between_bwd = (chip < src[None, :]) & (src[None, :] < src[:, None])
    sum_fwd = jnp.sum(jnp.where(between_fwd[:, :, None], all_t[None, :, :], 0.0), axis=1)
    sum_bwd = jnp.sum(jnp.where(between_bwd[:, :, None], all_t[None, :, :], 0.0), axis=1)
    w_fwd = jnp.where((src < chip)[:, None], jnp.exp(sum_fwd), 0.0)
    w_bwd = jnp.where((src > chip)[:, None], jnp.exp(sum_bwd), 0.0)
    pre_x = jnp.einsum("ch,chpn->hpn", w_fwd, all_x, precision=highest)
    pre_y = jnp.einsum("ch,chpn->hpn", w_bwd, all_y, precision=highest)
    joined_x = join(pre_x, x_first, t_first)
    joined_y = join(pre_y, y_second, t_second)
    keep_x, send_x = pick(is_first, pre_x, joined_x), pick(is_first, joined_x, pre_x)
    keep_y, send_y = pick(is_first, joined_y, pre_y), pick(is_first, pre_y, joined_y)
    back = lax.ppermute(
        jnp.concatenate([send_x.reshape(rows, state_width), send_y.reshape(rows, state_width)]),
        "core",
        swap,
    )
    recv_x = back[:rows].reshape(half, width, state_width)
    recv_y = back[rows:].reshape(half, width, state_width)
    state_in = jnp.concatenate([pick(is_first, keep_x, recv_x), pick(is_first, recv_x, keep_x)])
    state_grad = jnp.concatenate([pick(is_first, keep_y, recv_y), pick(is_first, recv_y, keep_y)])
    return state_in, state_grad


def per_device(
    head_inputs, input_proj, output_mapping, decay_codes, boundary, head_decay_speeds, out_grad
):
    tok_count = head_inputs.shape[0]
    head_count = decay_codes.shape[0]
    head_width = head_inputs.shape[1] // head_count
    state_width = input_proj.shape[1]
    increment_length = step_table(decay_codes)
    logarithm_decay = (
        -head_decay_speeds[:, None] * increment_length
        - sudden_falloff * boundary.astype(jnp.float32)[None, :]
    )
    cumul = jnp.cumsum(logarithm_decay, axis=1)
    group_total = cumul[:, -1]
    to_end = spread_heads(jnp.exp(group_total[:, None] - cumul), head_width)
    from_start = spread_heads(jnp.exp(cumul), head_width)
    scaled_in = head_inputs * spread_heads(increment_length, head_width)
    weighted_in = scaled_in * to_end
    weighted_grad = out_grad * from_start
    ends = jnp.einsum("tk,tn->kn", weighted_in, input_proj, precision=highest)
    starts = jnp.einsum("tk,tn->kn", weighted_grad, output_mapping, precision=highest)
    state_in, state_grad = chip_scans(
        ends.reshape(head_count, head_width, state_width),
        starts.reshape(head_count, head_width, state_width),
        group_total,
    )

    scores_t = jnp.einsum("sn,tn->st", input_proj, output_mapping, precision=highest)
    grad_scaled, grad_scores_t = block_terms(cumul, scores_t, scaled_in, out_grad)
    block_b = jnp.dot(grad_scores_t, output_mapping, precision=highest)
    block_c = jnp.einsum("st,sn->tn", grad_scores_t, input_proj, precision=highest)

    flat_in = state_in.reshape(head_count * head_width, state_width)
    flat_grad = state_grad.reshape(head_count * head_width, state_width)
    carry_c = jnp.dot(weighted_grad, flat_in, precision=highest)
    carry_b = jnp.dot(weighted_in, flat_grad, precision=highest)
    carry_x = to_end * jnp.einsum("tn,kn->tk", input_proj, flat_grad, precision=highest)
    grad_inputs = (grad_scaled + carry_x) * spread_heads(increment_length, head_width)

    both = jnp.concatenate([block_b + carry_b, block_c + carry_c], axis=1)
    parts = lax.axis_size("head")
    spread = lax.all_to_all(both, "head", 0, 0, tiled=True)
    summed = spread.reshape(parts, tok_count // parts, 2 * state_width).sum(axis=0)
    return (grad_inputs, summed[:, :state_width], summed[:, state_width:])


def solution(mesh):
    seq_count, head_parts = mesh.devices.shape
    split = jax.sharding.Mesh(
        mesh.devices.reshape(seq_count // 2, 2, head_parts), ("z", "core", "head")
    )
    seq = ("z", "core")
    return jax.shard_map(
        per_device,
        mesh=split,
        in_specs=(
            P(seq, "head"),
            P(seq, None),
            P(seq, None),
            P("head", seq),
            P(seq),
            P("head"),
            P(seq, "head"),
        ),
        out_specs=(P(seq, "head"), P(("z", "core", "head"), None), P(("z", "core", "head"), None)),
        check_vma=False,
    )
```

```python
import jax
import jax.numpy as jnp
from jax import lax
from jax.experimental import pallas as pl
from jax.experimental.pallas import tpu as pltpu
from jax.sharding import PartitionSpec as P

sudden_falloff = 0.35
highest = lax.Precision.HIGHEST
HEADS_PER_STEP = 2


def step_table(decay_codes):
    levels = jnp.arange(16, dtype=jnp.int32)
    values = 0.5 * 4.0 ** (levels.astype(jnp.float32) / 15.0)
    matching_label = decay_codes[None, :, :] == levels[:, None, None]
    return jnp.sum(jnp.where(matching_label, values[:, None, None], 0.0), axis=0)


def spread_heads(per_head, head_width):
    head_count, tok_count = per_head.shape
    wide = jnp.broadcast_to(per_head.T[:, :, None], (tok_count, head_count, head_width))
    return wide.reshape(tok_count, head_count * head_width)


def block_kernel(cum_row_ref, cum_col_ref, scores_t_ref, in_ref, grad_ref, flow_ref, acc_ref):
    step = pl.program_id(0)

    @pl.when(step == 0)
    def _():
        acc_ref[...] = jnp.zeros_like(acc_ref)

    tok = scores_t_ref.shape[0]
    width = in_ref.shape[1] // HEADS_PER_STEP
    rows = lax.broadcasted_iota(jnp.int32, (tok, tok), 0)
    cols = lax.broadcasted_iota(jnp.int32, (tok, tok), 1)
    later = cols >= rows
    scores_t = scores_t_ref[...]
    for k in range(HEADS_PER_STEP):
        gap = cum_row_ref[k] - cum_col_ref[k]
        decay_t = jnp.where(later, jnp.exp(jnp.where(later, gap, 0.0)), 0.0)
        own_in = in_ref[:, k * width:(k + 1) * width]
        own_grad = grad_ref[:, k * width:(k + 1) * width]
        flow_ref[:, k * width:(k + 1) * width] = jnp.dot(
            scores_t * decay_t, own_grad, precision=highest, preferred_element_type=jnp.float32
        )
        pair_t = lax.dot_general(
            own_in, own_grad, (((1,), (1,)), ((), ())), precision=highest,
            preferred_element_type=jnp.float32,
        )
        acc_ref[...] += pair_t * decay_t


def block_terms(cumul, scores_t, scaled_in, out_grad):
    head_count, tok = cumul.shape
    chan = scaled_in.shape[1]
    lanes = chan // head_count * HEADS_PER_STEP
    cum_row = cumul.reshape(head_count, 1, tok)
    cum_col = cumul.reshape(head_count, tok, 1)
    return pl.pallas_call(
        block_kernel,
        grid=(head_count // HEADS_PER_STEP,),
        in_specs=[
            pl.BlockSpec((HEADS_PER_STEP, 1, tok), lambda j: (j, 0, 0)),
            pl.BlockSpec((HEADS_PER_STEP, tok, 1), lambda j: (j, 0, 0)),
            pl.BlockSpec((tok, tok), lambda j: (0, 0)),
            pl.BlockSpec((tok, lanes), lambda j: (0, j)),
            pl.BlockSpec((tok, lanes), lambda j: (0, j)),
        ],
        out_specs=[
            pl.BlockSpec((tok, lanes), lambda j: (0, j)),
            pl.BlockSpec((tok, tok), lambda j: (0, 0)),
        ],
        out_shape=[
            jax.ShapeDtypeStruct((tok, chan), jnp.float32),
            jax.ShapeDtypeStruct((tok, tok), jnp.float32),
        ],
    )(cum_row, cum_col, scores_t, scaled_in, out_grad)


def pack_total(total, state_width):
    head_count = total.shape[0]
    rows = jnp.zeros((8, state_width), jnp.float32)
    return lax.dynamic_update_slice(
        rows, jnp.broadcast_to(total[:, None], (head_count, state_width)), (0, 0)
    )


def join(earlier, later, later_total):
    return jnp.exp(later_total)[:, None, None] * earlier + later


def pick(flag, when_true, when_false):
    return jnp.where(flag, when_true, when_false)


def chip_scans(ends, starts, total):
    chips = lax.axis_size("z")
    chip = lax.axis_index("z")
    core = lax.axis_index("core")
    head_count, width, state_width = ends.shape
    half = head_count // 2
    rows = half * width
    swap = [(0, 1), (1, 0)]
    mine_lo = core * half
    other_lo = (1 - core) * half

    def heads(value, lo):
        return lax.dynamic_slice_in_dim(value, lo, half, 0)

    own_x, own_y, own_t = heads(ends, mine_lo), heads(starts, mine_lo), heads(total, mine_lo)
    outgoing = jnp.concatenate(
        [
            heads(ends, other_lo).reshape(rows, state_width),
            heads(starts, other_lo).reshape(rows, state_width),
            pack_total(heads(total, other_lo), state_width),
        ],
        axis=0,
    )
    incoming = lax.ppermute(outgoing, "core", swap)
    got_x = incoming[:rows].reshape(half, width, state_width)
    got_y = incoming[rows:2 * rows].reshape(half, width, state_width)
    got_t = incoming[2 * rows:2 * rows + half, 0]
    is_first = core == 0
    x_first, x_second = pick(is_first, own_x, got_x), pick(is_first, got_x, own_x)
    y_first, y_second = pick(is_first, own_y, got_y), pick(is_first, got_y, own_y)
    t_first, t_second = pick(is_first, own_t, got_t), pick(is_first, got_t, own_t)
    chip_x = join(x_first, x_second, t_second)
    chip_y = join(y_second, y_first, t_first)
    chip_t = t_first + t_second
    gathered = lax.all_gather(
        jnp.concatenate(
            [
                chip_x.reshape(rows, state_width),
                chip_y.reshape(rows, state_width),
                pack_total(chip_t, state_width),
            ],
            axis=0,
        ),
        "z",
    )
    all_t = gathered[:, 2 * rows:2 * rows + half, 0]
    src = jnp.arange(chips, dtype=jnp.int32)
    between_fwd = (src[:, None] < src[None, :]) & (src[None, :] < chip)
    between_bwd = (chip < src[None, :]) & (src[None, :] < src[:, None])
    sum_fwd = jnp.sum(jnp.where(between_fwd[:, :, None], all_t[None, :, :], 0.0), axis=1)
    sum_bwd = jnp.sum(jnp.where(between_bwd[:, :, None], all_t[None, :, :], 0.0), axis=1)
    w_fwd = jnp.where((src < chip)[:, None], jnp.exp(sum_fwd), 0.0)
    w_bwd = jnp.where((src > chip)[:, None], jnp.exp(sum_bwd), 0.0)
    row_weights = jnp.concatenate(
        [
            jnp.repeat(w_fwd, width, axis=1),
            jnp.repeat(w_bwd, width, axis=1),
            jnp.zeros((chips, gathered.shape[1] - 2 * rows), jnp.float32),
        ],
        axis=1,
    )
    summed = jnp.sum(row_weights[:, :, None] * gathered, axis=0)
    pre_x = summed[:rows].reshape(half, width, state_width)
    pre_y = summed[rows:2 * rows].reshape(half, width, state_width)
    joined_x = join(pre_x, x_first, t_first)
    joined_y = join(pre_y, y_second, t_second)
    keep_x, send_x = pick(is_first, pre_x, joined_x), pick(is_first, joined_x, pre_x)
    keep_y, send_y = pick(is_first, joined_y, pre_y), pick(is_first, pre_y, joined_y)
    back = lax.ppermute(
        jnp.concatenate([send_x.reshape(rows, state_width), send_y.reshape(rows, state_width)]),
        "core",
        swap,
    )
    recv_x = back[:rows].reshape(half, width, state_width)
    recv_y = back[rows:].reshape(half, width, state_width)
    state_in = jnp.concatenate([pick(is_first, keep_x, recv_x), pick(is_first, recv_x, keep_x)])
    state_grad = jnp.concatenate([pick(is_first, keep_y, recv_y), pick(is_first, recv_y, keep_y)])
    return state_in, state_grad


def per_device(
    head_inputs, input_proj, output_mapping, decay_codes, boundary, head_decay_speeds, out_grad
):
    tok_count = head_inputs.shape[0]
    head_count = decay_codes.shape[0]
    head_width = head_inputs.shape[1] // head_count
    state_width = input_proj.shape[1]
    increment_length = step_table(decay_codes)
    logarithm_decay = (
        -head_decay_speeds[:, None] * increment_length
        - sudden_falloff * boundary.astype(jnp.float32)[None, :]
    )
    cumul = jnp.cumsum(logarithm_decay, axis=1)
    group_total = cumul[:, -1]
    to_end = spread_heads(jnp.exp(group_total[:, None] - cumul), head_width)
    from_start = spread_heads(jnp.exp(cumul), head_width)
    scaled_in = head_inputs * spread_heads(increment_length, head_width)
    weighted_in = scaled_in * to_end
    weighted_grad = out_grad * from_start
    ends = jnp.einsum("tk,tn->kn", weighted_in, input_proj, precision=highest)
    starts = jnp.einsum("tk,tn->kn", weighted_grad, output_mapping, precision=highest)
    state_in, state_grad = chip_scans(
        ends.reshape(head_count, head_width, state_width),
        starts.reshape(head_count, head_width, state_width),
        group_total,
    )

    scores_t = jnp.einsum("sn,tn->st", input_proj, output_mapping, precision=highest)
    grad_scaled, grad_scores_t = block_terms(cumul, scores_t, scaled_in, out_grad)
    block_b = jnp.dot(grad_scores_t, output_mapping, precision=highest)
    block_c = jnp.einsum("st,sn->tn", grad_scores_t, input_proj, precision=highest)

    flat_in = state_in.reshape(head_count * head_width, state_width)
    flat_grad = state_grad.reshape(head_count * head_width, state_width)
    carry_c = jnp.dot(weighted_grad, flat_in, precision=highest)
    carry_b = jnp.dot(weighted_in, flat_grad, precision=highest)
    carry_x = to_end * jnp.einsum("tn,kn->tk", input_proj, flat_grad, precision=highest)
    grad_inputs = (grad_scaled + carry_x) * spread_heads(increment_length, head_width)

    both = jnp.concatenate([block_b + carry_b, block_c + carry_c], axis=1)
    parts = lax.axis_size("head")
    spread = lax.all_to_all(both, "head", 0, 0, tiled=True)
    summed = spread.reshape(parts, tok_count // parts, 2 * state_width).sum(axis=0)
    return (grad_inputs, summed[:, :state_width], summed[:, state_width:])


def solution(mesh):
    seq_count, head_parts = mesh.devices.shape
    split = jax.sharding.Mesh(
        mesh.devices.reshape(seq_count // 2, 2, head_parts), ("z", "core", "head")
    )
    seq = ("z", "core")
    return jax.shard_map(
        per_device,
        mesh=split,
        in_specs=(
            P(seq, "head"),
            P(seq, None),
            P(seq, None),
            P("head", seq),
            P(seq),
            P("head"),
            P(seq, "head"),
        ),
        out_specs=(P(seq, "head"), P(("z", "core", "head"), None), P(("z", "core", "head"), None)),
        check_vma=False,
    )
```

```python
import jax
import jax.numpy as jnp
from jax import lax
from jax.experimental import pallas as pl
from jax.experimental.pallas import tpu as pltpu
from jax.sharding import PartitionSpec as P

sudden_falloff = 0.35
highest = lax.Precision.HIGHEST
HEADS_PER_STEP = 2


def step_table(decay_codes):
    levels = jnp.arange(16, dtype=jnp.int32)
    values = 0.5 * 4.0 ** (levels.astype(jnp.float32) / 15.0)
    matching_label = decay_codes[None, :, :] == levels[:, None, None]
    return jnp.sum(jnp.where(matching_label, values[:, None, None], 0.0), axis=0)


def spread_heads(per_head, head_width):
    head_count, tok_count = per_head.shape
    wide = jnp.broadcast_to(per_head.T[:, :, None], (tok_count, head_count, head_width))
    return wide.reshape(tok_count, head_count * head_width)


def block_kernel(cum_row_ref, cum_col_ref, scores_t_ref, in_ref, grad_ref, flow_ref, acc_ref):
    step = pl.program_id(0)

    @pl.when(step == 0)
    def _():
        acc_ref[...] = jnp.zeros_like(acc_ref)

    tok = scores_t_ref.shape[0]
    width = in_ref.shape[1] // HEADS_PER_STEP
    rows = lax.broadcasted_iota(jnp.int32, (tok, tok), 0)
    cols = lax.broadcasted_iota(jnp.int32, (tok, tok), 1)
    later = cols >= rows
    scores_t = scores_t_ref[...]
    for k in range(HEADS_PER_STEP):
        gap = cum_row_ref[k] - cum_col_ref[k]
        decay_t = jnp.where(later, jnp.exp(jnp.where(later, gap, 0.0)), 0.0)
        own_in = in_ref[:, k * width:(k + 1) * width]
        own_grad = grad_ref[:, k * width:(k + 1) * width]
        flow_ref[:, k * width:(k + 1) * width] = jnp.dot(
            scores_t * decay_t, own_grad, precision=highest, preferred_element_type=jnp.float32
        )
        pair_t = lax.dot_general(
            own_in, own_grad, (((1,), (1,)), ((), ())), precision=highest,
            preferred_element_type=jnp.float32,
        )
        acc_ref[...] += pair_t * decay_t


def block_terms(cumul, scores_t, scaled_in, out_grad):
    head_count, tok = cumul.shape
    chan = scaled_in.shape[1]
    lanes = chan // head_count * HEADS_PER_STEP
    cum_row = cumul.reshape(head_count, 1, tok)
    cum_col = cumul.reshape(head_count, tok, 1)
    return pl.pallas_call(
        block_kernel,
        grid=(head_count // HEADS_PER_STEP,),
        in_specs=[
            pl.BlockSpec((HEADS_PER_STEP, 1, tok), lambda j: (j, 0, 0)),
            pl.BlockSpec((HEADS_PER_STEP, tok, 1), lambda j: (j, 0, 0)),
            pl.BlockSpec((tok, tok), lambda j: (0, 0)),
            pl.BlockSpec((tok, lanes), lambda j: (0, j)),
            pl.BlockSpec((tok, lanes), lambda j: (0, j)),
        ],
        out_specs=[
            pl.BlockSpec((tok, lanes), lambda j: (0, j)),
            pl.BlockSpec((tok, tok), lambda j: (0, 0)),
        ],
        out_shape=[
            jax.ShapeDtypeStruct((tok, chan), jnp.float32),
            jax.ShapeDtypeStruct((tok, tok), jnp.float32),
        ],
    )(cum_row, cum_col, scores_t, scaled_in, out_grad)


def pack_total(total, state_width):
    head_count = total.shape[0]
    rows = jnp.zeros((8, state_width), jnp.float32)
    return lax.dynamic_update_slice(
        rows, jnp.broadcast_to(total[:, None], (head_count, state_width)), (0, 0)
    )


def join(earlier, later, later_total):
    return jnp.exp(later_total)[:, None, None] * earlier + later


def pick(flag, when_true, when_false):
    return jnp.where(flag, when_true, when_false)


def chip_scans(ends, starts, total):
    chips = lax.axis_size("z")
    chip = lax.axis_index("z")
    core = lax.axis_index("core")
    head_count, width, state_width = ends.shape
    half = head_count // 2
    rows = half * width
    swap = [(0, 1), (1, 0)]
    mine_lo = core * half
    other_lo = (1 - core) * half

    def heads(value, lo):
        return lax.dynamic_slice_in_dim(value, lo, half, 0)

    own_x, own_y, own_t = heads(ends, mine_lo), heads(starts, mine_lo), heads(total, mine_lo)
    outgoing = jnp.concatenate(
        [
            heads(ends, other_lo).reshape(rows, state_width),
            heads(starts, other_lo).reshape(rows, state_width),
            pack_total(heads(total, other_lo), state_width),
        ],
        axis=0,
    )
    incoming = lax.ppermute(outgoing, "core", swap)
    got_x = incoming[:rows].reshape(half, width, state_width)
    got_y = incoming[rows:2 * rows].reshape(half, width, state_width)
    got_t = incoming[2 * rows:2 * rows + half, 0]
    is_first = core == 0
    x_first, x_second = pick(is_first, own_x, got_x), pick(is_first, got_x, own_x)
    y_first, y_second = pick(is_first, own_y, got_y), pick(is_first, got_y, own_y)
    t_first, t_second = pick(is_first, own_t, got_t), pick(is_first, got_t, own_t)
    chip_x = join(x_first, x_second, t_second)
    chip_y = join(y_second, y_first, t_first)
    chip_t = t_first + t_second
    gathered = lax.all_gather(
        jnp.concatenate(
            [
                chip_x.reshape(rows, state_width),
                chip_y.reshape(rows, state_width),
                pack_total(chip_t, state_width),
            ],
            axis=0,
        ),
        "z",
    )
    all_t = gathered[:, 2 * rows:2 * rows + half, 0]
    src = jnp.arange(chips, dtype=jnp.int32)
    between_fwd = (src[:, None] < src[None, :]) & (src[None, :] < chip)
    between_bwd = (chip < src[None, :]) & (src[None, :] < src[:, None])
    sum_fwd = jnp.sum(jnp.where(between_fwd[:, :, None], all_t[None, :, :], 0.0), axis=1)
    sum_bwd = jnp.sum(jnp.where(between_bwd[:, :, None], all_t[None, :, :], 0.0), axis=1)
    w_fwd = jnp.where((src < chip)[:, None], jnp.exp(sum_fwd), 0.0)
    w_bwd = jnp.where((src > chip)[:, None], jnp.exp(sum_bwd), 0.0)
    weights = jnp.stack([w_fwd, w_bwd], axis=1)
    blocks = gathered[:, :2 * rows].reshape(chips, 2, half, width, state_width)
    summed = jnp.sum(weights[:, :, :, None, None] * blocks, axis=0)
    pre_x = summed[0]
    pre_y = summed[1]
    joined_x = join(pre_x, x_first, t_first)
    joined_y = join(pre_y, y_second, t_second)
    keep_x, send_x = pick(is_first, pre_x, joined_x), pick(is_first, joined_x, pre_x)
    keep_y, send_y = pick(is_first, joined_y, pre_y), pick(is_first, pre_y, joined_y)
    back = lax.ppermute(
        jnp.concatenate([send_x.reshape(rows, state_width), send_y.reshape(rows, state_width)]),
        "core",
        swap,
    )
    recv_x = back[:rows].reshape(half, width, state_width)
    recv_y = back[rows:].reshape(half, width, state_width)
    state_in = jnp.concatenate([pick(is_first, keep_x, recv_x), pick(is_first, recv_x, keep_x)])
    state_grad = jnp.concatenate([pick(is_first, keep_y, recv_y), pick(is_first, recv_y, keep_y)])
    return state_in, state_grad


def per_device(
    head_inputs, input_proj, output_mapping, decay_codes, boundary, head_decay_speeds, out_grad
):
    tok_count = head_inputs.shape[0]
    head_count = decay_codes.shape[0]
    head_width = head_inputs.shape[1] // head_count
    state_width = input_proj.shape[1]
    increment_length = step_table(decay_codes)
    logarithm_decay = (
        -head_decay_speeds[:, None] * increment_length
        - sudden_falloff * boundary.astype(jnp.float32)[None, :]
    )
    cumul = jnp.cumsum(logarithm_decay, axis=1)
    group_total = cumul[:, -1]
    to_end = spread_heads(jnp.exp(group_total[:, None] - cumul), head_width)
    from_start = spread_heads(jnp.exp(cumul), head_width)
    scaled_in = head_inputs * spread_heads(increment_length, head_width)
    weighted_in = scaled_in * to_end
    weighted_grad = out_grad * from_start
    ends = jnp.einsum("tk,tn->kn", weighted_in, input_proj, precision=highest)
    starts = jnp.einsum("tk,tn->kn", weighted_grad, output_mapping, precision=highest)
    state_in, state_grad = chip_scans(
        ends.reshape(head_count, head_width, state_width),
        starts.reshape(head_count, head_width, state_width),
        group_total,
    )

    scores_t = jnp.einsum("sn,tn->st", input_proj, output_mapping, precision=highest)
    grad_scaled, grad_scores_t = block_terms(cumul, scores_t, scaled_in, out_grad)
    block_b = jnp.dot(grad_scores_t, output_mapping, precision=highest)
    block_c = jnp.einsum("st,sn->tn", grad_scores_t, input_proj, precision=highest)

    flat_in = state_in.reshape(head_count * head_width, state_width)
    flat_grad = state_grad.reshape(head_count * head_width, state_width)
    carry_c = jnp.dot(weighted_grad, flat_in, precision=highest)
    carry_b = jnp.dot(weighted_in, flat_grad, precision=highest)
    carry_x = to_end * jnp.einsum("tn,kn->tk", input_proj, flat_grad, precision=highest)
    grad_inputs = (grad_scaled + carry_x) * spread_heads(increment_length, head_width)

    both = jnp.concatenate([block_b + carry_b, block_c + carry_c], axis=1)
    parts = lax.axis_size("head")
    spread = lax.all_to_all(both, "head", 0, 0, tiled=True)
    summed = spread.reshape(parts, tok_count // parts, 2 * state_width).sum(axis=0)
    return (grad_inputs, summed[:, :state_width], summed[:, state_width:])


def solution(mesh):
    seq_count, head_parts = mesh.devices.shape
    split = jax.sharding.Mesh(
        mesh.devices.reshape(seq_count // 2, 2, head_parts), ("z", "core", "head")
    )
    seq = ("z", "core")
    return jax.shard_map(
        per_device,
        mesh=split,
        in_specs=(
            P(seq, "head"),
            P(seq, None),
            P(seq, None),
            P("head", seq),
            P(seq),
            P("head"),
            P(seq, "head"),
        ),
        out_specs=(P(seq, "head"), P(("z", "core", "head"), None), P(("z", "core", "head"), None)),
        check_vma=False,
    )
```

```python
import jax
import jax.numpy as jnp
from jax import lax
from jax.experimental import pallas as pl
from jax.experimental.pallas import tpu as pltpu
from jax.sharding import PartitionSpec as P

sudden_falloff = 0.35
highest = lax.Precision.HIGHEST
HEADS_PER_STEP = 2


def step_table(decay_codes):
    levels = jnp.arange(16, dtype=jnp.int32)
    values = 0.5 * 4.0 ** (levels.astype(jnp.float32) / 15.0)
    matching_label = decay_codes[None, :, :] == levels[:, None, None]
    return jnp.sum(jnp.where(matching_label, values[:, None, None], 0.0), axis=0)


def spread_heads(per_head, head_width):
    head_count, tok_count = per_head.shape
    wide = jnp.broadcast_to(per_head.T[:, :, None], (tok_count, head_count, head_width))
    return wide.reshape(tok_count, head_count * head_width)


def block_kernel(cum_row_ref, cum_col_ref, scores_t_ref, in_ref, grad_ref, flow_ref, acc_ref):
    step = pl.program_id(0)

    @pl.when(step == 0)
    def _():
        acc_ref[...] = jnp.zeros_like(acc_ref)

    tok = scores_t_ref.shape[0]
    width = in_ref.shape[1] // HEADS_PER_STEP
    rows = lax.broadcasted_iota(jnp.int32, (tok, tok), 0)
    cols = lax.broadcasted_iota(jnp.int32, (tok, tok), 1)
    later = cols >= rows
    scores_t = scores_t_ref[...]
    for k in range(HEADS_PER_STEP):
        gap = cum_row_ref[k] - cum_col_ref[k]
        decay_t = jnp.where(later, jnp.exp(jnp.where(later, gap, 0.0)), 0.0)
        own_in = in_ref[:, k * width:(k + 1) * width]
        own_grad = grad_ref[:, k * width:(k + 1) * width]
        flow_ref[:, k * width:(k + 1) * width] = jnp.dot(
            scores_t * decay_t, own_grad, precision=highest, preferred_element_type=jnp.float32
        )
        pair_t = lax.dot_general(
            own_in, own_grad, (((1,), (1,)), ((), ())), precision=highest,
            preferred_element_type=jnp.float32,
        )
        acc_ref[...] += pair_t * decay_t


def block_terms(cumul, scores_t, scaled_in, out_grad):
    head_count, tok = cumul.shape
    chan = scaled_in.shape[1]
    lanes = chan // head_count * HEADS_PER_STEP
    cum_row = cumul.reshape(head_count, 1, tok)
    cum_col = cumul.reshape(head_count, tok, 1)
    return pl.pallas_call(
        block_kernel,
        grid=(head_count // HEADS_PER_STEP,),
        in_specs=[
            pl.BlockSpec((HEADS_PER_STEP, 1, tok), lambda j: (j, 0, 0)),
            pl.BlockSpec((HEADS_PER_STEP, tok, 1), lambda j: (j, 0, 0)),
            pl.BlockSpec((tok, tok), lambda j: (0, 0)),
            pl.BlockSpec((tok, lanes), lambda j: (0, j)),
            pl.BlockSpec((tok, lanes), lambda j: (0, j)),
        ],
        out_specs=[
            pl.BlockSpec((tok, lanes), lambda j: (0, j)),
            pl.BlockSpec((tok, tok), lambda j: (0, 0)),
        ],
        out_shape=[
            jax.ShapeDtypeStruct((tok, chan), jnp.float32),
            jax.ShapeDtypeStruct((tok, tok), jnp.float32),
        ],
    )(cum_row, cum_col, scores_t, scaled_in, out_grad)


def pack_total(total, state_width):
    head_count = total.shape[0]
    rows = jnp.zeros((8, state_width), jnp.float32)
    return lax.dynamic_update_slice(
        rows, jnp.broadcast_to(total[:, None], (head_count, state_width)), (0, 0)
    )


def join(earlier, later, later_total):
    return jnp.exp(later_total)[:, None, None] * earlier + later


def pick(flag, when_true, when_false):
    return jnp.where(flag, when_true, when_false)


def chip_scans(ends, starts, total):
    chips = lax.axis_size("z")
    core = lax.axis_index("core")
    head_count, width, state_width = ends.shape
    rows = head_count * width
    both = ("z", "core")
    swap = [(0, 1), (1, 0)]
    is_fwd = core == 0
    tot_rows = pack_total(total, state_width)
    mine = pick(is_fwd, ends, starts)
    outgoing = jnp.concatenate(
        [pick(is_fwd, starts, ends).reshape(rows, state_width), tot_rows], axis=0
    )
    incoming = lax.ppermute(outgoing, "core", swap)
    partner = incoming[:rows].reshape(head_count, width, state_width)
    partner_t = incoming[rows:rows + head_count, 0]
    chip_state = join(mine, partner, partner_t)
    chip_t = total + partner_t

    def packed(state, tot):
        return jnp.concatenate(
            [state.reshape(rows, state_width), pack_total(tot, state_width)], axis=0
        )

    def unpacked(value):
        return value[:rows].reshape(head_count, width, state_width), value[rows:rows + head_count, 0]

    def move(value, hop):
        pairs = []
        for z in range(chips):
            if z + hop < chips:
                pairs.append((2 * z, 2 * (z + hop)))
            if z - hop >= 0:
                pairs.append((2 * z + 1, 2 * (z - hop) + 1))
        return lax.ppermute(value, both, pairs)

    running = move(packed(chip_state, chip_t), 1)
    hop = 1
    while hop < chips:
        got_state, got_t = unpacked(move(running, hop))
        run_state, run_t = unpacked(running)
        running = packed(join(got_state, run_state, run_t), got_t + run_t)
        hop *= 2
    prefix, unused = unpacked(running)
    joined = join(prefix, mine, total)
    back = lax.ppermute(joined.reshape(rows, state_width), "core", swap)
    other = back.reshape(head_count, width, state_width)
    state_in = pick(is_fwd, prefix, other)
    state_grad = pick(is_fwd, other, prefix)
    return state_in, state_grad


def per_device(
    head_inputs, input_proj, output_mapping, decay_codes, boundary, head_decay_speeds, out_grad
):
    tok_count = head_inputs.shape[0]
    head_count = decay_codes.shape[0]
    head_width = head_inputs.shape[1] // head_count
    state_width = input_proj.shape[1]
    increment_length = step_table(decay_codes)
    logarithm_decay = (
        -head_decay_speeds[:, None] * increment_length
        - sudden_falloff * boundary.astype(jnp.float32)[None, :]
    )
    cumul = jnp.cumsum(logarithm_decay, axis=1)
    group_total = cumul[:, -1]
    to_end = spread_heads(jnp.exp(group_total[:, None] - cumul), head_width)
    from_start = spread_heads(jnp.exp(cumul), head_width)
    scaled_in = head_inputs * spread_heads(increment_length, head_width)
    weighted_in = scaled_in * to_end
    weighted_grad = out_grad * from_start
    ends = jnp.einsum("tk,tn->kn", weighted_in, input_proj, precision=highest)
    starts = jnp.einsum("tk,tn->kn", weighted_grad, output_mapping, precision=highest)
    state_in, state_grad = chip_scans(
        ends.reshape(head_count, head_width, state_width),
        starts.reshape(head_count, head_width, state_width),
        group_total,
    )

    scores_t = jnp.einsum("sn,tn->st", input_proj, output_mapping, precision=highest)
    grad_scaled, grad_scores_t = block_terms(cumul, scores_t, scaled_in, out_grad)
    block_b = jnp.dot(grad_scores_t, output_mapping, precision=highest)
    block_c = jnp.einsum("st,sn->tn", grad_scores_t, input_proj, precision=highest)

    flat_in = state_in.reshape(head_count * head_width, state_width)
    flat_grad = state_grad.reshape(head_count * head_width, state_width)
    carry_c = jnp.dot(weighted_grad, flat_in, precision=highest)
    carry_b = jnp.dot(weighted_in, flat_grad, precision=highest)
    carry_x = to_end * jnp.einsum("tn,kn->tk", input_proj, flat_grad, precision=highest)
    grad_inputs = (grad_scaled + carry_x) * spread_heads(increment_length, head_width)

    both = jnp.concatenate([block_b + carry_b, block_c + carry_c], axis=1)
    parts = lax.axis_size("head")
    spread = lax.all_to_all(both, "head", 0, 0, tiled=True)
    summed = spread.reshape(parts, tok_count // parts, 2 * state_width).sum(axis=0)
    return (grad_inputs, summed[:, :state_width], summed[:, state_width:])


def solution(mesh):
    seq_count, head_parts = mesh.devices.shape
    split = jax.sharding.Mesh(
        mesh.devices.reshape(seq_count // 2, 2, head_parts), ("z", "core", "head")
    )
    seq = ("z", "core")
    return jax.shard_map(
        per_device,
        mesh=split,
        in_specs=(
            P(seq, "head"),
            P(seq, None),
            P(seq, None),
            P("head", seq),
            P(seq),
            P("head"),
            P(seq, "head"),
        ),
        out_specs=(P(seq, "head"), P(("z", "core", "head"), None), P(("z", "core", "head"), None)),
        check_vma=False,
    )
```

```python
import jax
import jax.numpy as jnp
from jax import lax
from jax.experimental import pallas as pl
from jax.experimental.pallas import tpu as pltpu
from jax.sharding import PartitionSpec as P

sudden_falloff = 0.35
highest = lax.Precision.HIGHEST
HEADS_PER_STEP = 2


def step_table(decay_codes):
    levels = jnp.arange(16, dtype=jnp.int32)
    values = 0.5 * 4.0 ** (levels.astype(jnp.float32) / 15.0)
    matching_label = decay_codes[None, :, :] == levels[:, None, None]
    return jnp.sum(jnp.where(matching_label, values[:, None, None], 0.0), axis=0)


def spread_heads(per_head, head_width):
    head_count, tok_count = per_head.shape
    wide = jnp.broadcast_to(per_head.T[:, :, None], (tok_count, head_count, head_width))
    return wide.reshape(tok_count, head_count * head_width)


def block_kernel(cum_row_ref, cum_col_ref, scores_t_ref, in_ref, grad_ref, flow_ref, acc_ref):
    step = pl.program_id(0)

    @pl.when(step == 0)
    def _():
        acc_ref[...] = jnp.zeros_like(acc_ref)

    tok = scores_t_ref.shape[0]
    width = in_ref.shape[1] // HEADS_PER_STEP
    rows = lax.broadcasted_iota(jnp.int32, (tok, tok), 0)
    cols = lax.broadcasted_iota(jnp.int32, (tok, tok), 1)
    later = cols >= rows
    scores_t = scores_t_ref[...]
    for k in range(HEADS_PER_STEP):
        gap = cum_row_ref[k] - cum_col_ref[k]
        decay_t = jnp.where(later, jnp.exp(jnp.where(later, gap, 0.0)), 0.0)
        own_in = in_ref[:, k * width:(k + 1) * width]
        own_grad = grad_ref[:, k * width:(k + 1) * width]
        flow_ref[:, k * width:(k + 1) * width] = jnp.dot(
            scores_t * decay_t, own_grad, precision=highest, preferred_element_type=jnp.float32
        )
        pair_t = lax.dot_general(
            own_in, own_grad, (((1,), (1,)), ((), ())), precision=highest,
            preferred_element_type=jnp.float32,
        )
        acc_ref[...] += pair_t * decay_t


def block_terms(cumul, scores_t, scaled_in, out_grad):
    head_count, tok = cumul.shape
    chan = scaled_in.shape[1]
    lanes = chan // head_count * HEADS_PER_STEP
    cum_row = cumul.reshape(head_count, 1, tok)
    cum_col = cumul.reshape(head_count, tok, 1)
    return pl.pallas_call(
        block_kernel,
        grid=(head_count // HEADS_PER_STEP,),
        in_specs=[
            pl.BlockSpec((HEADS_PER_STEP, 1, tok), lambda j: (j, 0, 0)),
            pl.BlockSpec((HEADS_PER_STEP, tok, 1), lambda j: (j, 0, 0)),
            pl.BlockSpec((tok, tok), lambda j: (0, 0)),
            pl.BlockSpec((tok, lanes), lambda j: (0, j)),
            pl.BlockSpec((tok, lanes), lambda j: (0, j)),
        ],
        out_specs=[
            pl.BlockSpec((tok, lanes), lambda j: (0, j)),
            pl.BlockSpec((tok, tok), lambda j: (0, 0)),
        ],
        out_shape=[
            jax.ShapeDtypeStruct((tok, chan), jnp.float32),
            jax.ShapeDtypeStruct((tok, tok), jnp.float32),
        ],
    )(cum_row, cum_col, scores_t, scaled_in, out_grad)


def pack_total(total, state_width):
    head_count = total.shape[0]
    rows = jnp.zeros((8, state_width), jnp.float32)
    return lax.dynamic_update_slice(
        rows, jnp.broadcast_to(total[:, None], (head_count, state_width)), (0, 0)
    )


def join(earlier, later, later_total):
    return jnp.exp(later_total)[:, None, None] * earlier + later


def pick(flag, when_true, when_false):
    return jnp.where(flag, when_true, when_false)


def gathered_scans(ends, starts, total, hold):
    chips = lax.axis_size("z")
    chip = lax.axis_index("z")
    core = lax.axis_index("core")
    head_count, width, state_width = ends.shape
    half = head_count // 2
    rows = half * width
    swap = [(0, 1), (1, 0)]
    mine_lo = core * half
    other_lo = (1 - core) * half

    def heads(value, lo):
        return lax.dynamic_slice_in_dim(value, lo, half, 0)

    own_x, own_y, own_t = heads(ends, mine_lo), heads(starts, mine_lo), heads(total, mine_lo)
    outgoing = jnp.concatenate(
        [
            heads(ends, other_lo).reshape(rows, state_width),
            heads(starts, other_lo).reshape(rows, state_width),
            pack_total(heads(total, other_lo), state_width),
        ],
        axis=0,
    )
    incoming, held = hold(outgoing)
    got_x = incoming[:rows].reshape(half, width, state_width)
    got_y = incoming[rows:2 * rows].reshape(half, width, state_width)
    got_t = incoming[2 * rows:2 * rows + half, 0]
    is_first = core == 0
    x_first, x_second = pick(is_first, own_x, got_x), pick(is_first, got_x, own_x)
    y_first, y_second = pick(is_first, own_y, got_y), pick(is_first, got_y, own_y)
    t_first, t_second = pick(is_first, own_t, got_t), pick(is_first, got_t, own_t)
    chip_x = join(x_first, x_second, t_second)
    chip_y = join(y_second, y_first, t_first)
    chip_t = t_first + t_second
    payload, held = lax.optimization_barrier(
        (
            jnp.concatenate(
                [
                    chip_x.reshape(rows, state_width),
                    chip_y.reshape(rows, state_width),
                    pack_total(chip_t, state_width),
                ],
                axis=0,
            ),
            held,
        )
    )
    gathered = lax.all_gather(payload, "z")
    all_t = gathered[:, 2 * rows:2 * rows + half, 0]
    src = jnp.arange(chips, dtype=jnp.int32)
    between_fwd = (src[:, None] < src[None, :]) & (src[None, :] < chip)
    between_bwd = (chip < src[None, :]) & (src[None, :] < src[:, None])
    sum_fwd = jnp.sum(jnp.where(between_fwd[:, :, None], all_t[None, :, :], 0.0), axis=1)
    sum_bwd = jnp.sum(jnp.where(between_bwd[:, :, None], all_t[None, :, :], 0.0), axis=1)
    w_fwd = jnp.where((src < chip)[:, None], jnp.exp(sum_fwd), 0.0)
    w_bwd = jnp.where((src > chip)[:, None], jnp.exp(sum_bwd), 0.0)
    weights = jnp.stack([w_fwd, w_bwd], axis=1)
    blocks = gathered[:, :2 * rows].reshape(chips, 2, half, width, state_width)
    summed = jnp.sum(weights[:, :, :, None, None] * blocks, axis=0)
    pre_x = summed[0]
    pre_y = summed[1]
    joined_x = join(pre_x, x_first, t_first)
    joined_y = join(pre_y, y_second, t_second)
    keep_x, send_x = pick(is_first, pre_x, joined_x), pick(is_first, joined_x, pre_x)
    keep_y, send_y = pick(is_first, joined_y, pre_y), pick(is_first, pre_y, joined_y)
    back = lax.ppermute(
        jnp.concatenate([send_x.reshape(rows, state_width), send_y.reshape(rows, state_width)]),
        "core",
        swap,
    )
    recv_x = back[:rows].reshape(half, width, state_width)
    recv_y = back[rows:].reshape(half, width, state_width)
    state_in = jnp.concatenate([pick(is_first, keep_x, recv_x), pick(is_first, recv_x, keep_x)])
    state_grad = jnp.concatenate([pick(is_first, keep_y, recv_y), pick(is_first, recv_y, keep_y)])
    return state_in, state_grad, held


def stepped_scans(ends, starts, total, hold):
    chips = lax.axis_size("z")
    core = lax.axis_index("core")
    head_count, width, state_width = ends.shape
    rows = head_count * width
    both = ("z", "core")
    swap = [(0, 1), (1, 0)]
    is_fwd = core == 0
    tot_rows = pack_total(total, state_width)
    mine = pick(is_fwd, ends, starts)
    outgoing = jnp.concatenate(
        [pick(is_fwd, starts, ends).reshape(rows, state_width), tot_rows], axis=0
    )
    incoming = hold(outgoing)
    partner = incoming[:rows].reshape(head_count, width, state_width)
    partner_t = incoming[rows:rows + head_count, 0]
    chip_state = join(mine, partner, partner_t)
    chip_t = total + partner_t

    def packed(state, tot):
        return jnp.concatenate(
            [state.reshape(rows, state_width), pack_total(tot, state_width)], axis=0
        )

    def unpacked(value):
        return value[:rows].reshape(head_count, width, state_width), value[rows:rows + head_count, 0]

    def move(value, hop):
        pairs = []
        for z in range(chips):
            if z + hop < chips:
                pairs.append((2 * z, 2 * (z + hop)))
            if z - hop >= 0:
                pairs.append((2 * z + 1, 2 * (z - hop) + 1))
        return lax.ppermute(value, both, pairs)

    running = move(packed(chip_state, chip_t), 1)
    hop = 1
    while hop < chips:
        got_state, got_t = unpacked(move(running, hop))
        run_state, run_t = unpacked(running)
        running = packed(join(got_state, run_state, run_t), got_t + run_t)
        hop *= 2
    prefix, unused = unpacked(running)
    joined = join(prefix, mine, total)
    back = lax.ppermute(joined.reshape(rows, state_width), "core", swap)
    other = back.reshape(head_count, width, state_width)
    state_in = pick(is_fwd, prefix, other)
    state_grad = pick(is_fwd, other, prefix)
    return state_in, state_grad


def chip_scans(ends, starts, total):
    part = ends.shape[0] // 2
    state_width = ends.shape[2]
    box = {}

    def hold_b(outgoing):
        box["b"] = outgoing
        return box["b_in"]

    def hold_a(outgoing):
        rows_a = outgoing.shape[0]
        both = lax.ppermute(
            jnp.concatenate([outgoing, box["b"]], axis=0), "core", [(0, 1), (1, 0)]
        )
        box["b_in"] = both[rows_a:]
        return both[:rows_a], both[rows_a:]

    b_ends, b_starts, b_total = ends[part:], starts[part:], total[part:]
    core = lax.axis_index("core")
    rows_b = part * ends.shape[1]
    box["b"] = jnp.concatenate(
        [
            pick(core == 0, b_starts, b_ends).reshape(rows_b, state_width),
            pack_total(b_total, state_width),
        ],
        axis=0,
    )
    in_a, grad_a, held = gathered_scans(ends[:part], starts[:part], total[:part], hold_a)
    in_b, grad_b = stepped_scans(b_ends, b_starts, b_total, lambda unused: held)
    return jnp.concatenate([in_a, in_b]), jnp.concatenate([grad_a, grad_b])


def per_device(
    head_inputs, input_proj, output_mapping, decay_codes, boundary, head_decay_speeds, out_grad
):
    tok_count = head_inputs.shape[0]
    head_count = decay_codes.shape[0]
    head_width = head_inputs.shape[1] // head_count
    state_width = input_proj.shape[1]
    increment_length = step_table(decay_codes)
    logarithm_decay = (
        -head_decay_speeds[:, None] * increment_length
        - sudden_falloff * boundary.astype(jnp.float32)[None, :]
    )
    cumul = jnp.cumsum(logarithm_decay, axis=1)
    group_total = cumul[:, -1]
    to_end = spread_heads(jnp.exp(group_total[:, None] - cumul), head_width)
    from_start = spread_heads(jnp.exp(cumul), head_width)
    scaled_in = head_inputs * spread_heads(increment_length, head_width)
    weighted_in = scaled_in * to_end
    weighted_grad = out_grad * from_start
    ends = jnp.einsum("tk,tn->kn", weighted_in, input_proj, precision=highest)
    starts = jnp.einsum("tk,tn->kn", weighted_grad, output_mapping, precision=highest)
    state_in, state_grad = chip_scans(
        ends.reshape(head_count, head_width, state_width),
        starts.reshape(head_count, head_width, state_width),
        group_total,
    )

    scores_t = jnp.einsum("sn,tn->st", input_proj, output_mapping, precision=highest)
    grad_scaled, grad_scores_t = block_terms(cumul, scores_t, scaled_in, out_grad)
    block_b = jnp.dot(grad_scores_t, output_mapping, precision=highest)
    block_c = jnp.einsum("st,sn->tn", grad_scores_t, input_proj, precision=highest)

    flat_in = state_in.reshape(head_count * head_width, state_width)
    flat_grad = state_grad.reshape(head_count * head_width, state_width)
    carry_c = jnp.dot(weighted_grad, flat_in, precision=highest)
    carry_b = jnp.dot(weighted_in, flat_grad, precision=highest)
    carry_x = to_end * jnp.einsum("tn,kn->tk", input_proj, flat_grad, precision=highest)
    grad_inputs = (grad_scaled + carry_x) * spread_heads(increment_length, head_width)

    both = jnp.concatenate([block_b + carry_b, block_c + carry_c], axis=1)
    parts = lax.axis_size("head")
    spread = lax.all_to_all(both, "head", 0, 0, tiled=True)
    summed = spread.reshape(parts, tok_count // parts, 2 * state_width).sum(axis=0)
    return (grad_inputs, summed[:, :state_width], summed[:, state_width:])


def solution(mesh):
    seq_count, head_parts = mesh.devices.shape
    split = jax.sharding.Mesh(
        mesh.devices.reshape(seq_count // 2, 2, head_parts), ("z", "core", "head")
    )
    seq = ("z", "core")
    return jax.shard_map(
        per_device,
        mesh=split,
        in_specs=(
            P(seq, "head"),
            P(seq, None),
            P(seq, None),
            P("head", seq),
            P(seq),
            P("head"),
            P(seq, "head"),
        ),
        out_specs=(P(seq, "head"), P(("z", "core", "head"), None), P(("z", "core", "head"), None)),
        check_vma=False,
    )
```

```python
import jax
import jax.numpy as jnp
from jax import lax
from jax.experimental import pallas as pl
from jax.experimental.pallas import tpu as pltpu
from jax.sharding import PartitionSpec as P

sudden_falloff = 0.35
highest = lax.Precision.HIGHEST
HEADS_PER_STEP = 2


def step_table(decay_codes):
    levels = jnp.arange(16, dtype=jnp.int32)
    values = 0.5 * 4.0 ** (levels.astype(jnp.float32) / 15.0)
    matching_label = decay_codes[None, :, :] == levels[:, None, None]
    return jnp.sum(jnp.where(matching_label, values[:, None, None], 0.0), axis=0)


def spread_heads(per_head, head_width):
    head_count, tok_count = per_head.shape
    wide = jnp.broadcast_to(per_head.T[:, :, None], (tok_count, head_count, head_width))
    return wide.reshape(tok_count, head_count * head_width)


def block_kernel(cum_row_ref, cum_col_ref, scores_t_ref, in_ref, grad_ref, flow_ref, acc_ref):
    step = pl.program_id(0)

    @pl.when(step == 0)
    def _():
        acc_ref[...] = jnp.zeros_like(acc_ref)

    tok = scores_t_ref.shape[0]
    width = in_ref.shape[1] // HEADS_PER_STEP
    piece = 128
    for k in range(HEADS_PER_STEP):
        lanes = slice(k * width, (k + 1) * width)
        for first in range(0, tok, piece):
            span = tok - first
            rows = lax.broadcasted_iota(jnp.int32, (piece, span), 0)
            cols = lax.broadcasted_iota(jnp.int32, (piece, span), 1)
            later = cols >= rows
            gap = cum_row_ref[k, :, first:] - cum_col_ref[k, first:first + piece, :]
            decay_t = jnp.where(later, jnp.exp(jnp.where(later, gap, 0.0)), 0.0)
            own_in = in_ref[first:first + piece, lanes]
            own_grad = grad_ref[first:, lanes]
            flow_ref[first:first + piece, lanes] = jnp.dot(
                scores_t_ref[first:first + piece, first:] * decay_t, own_grad,
                precision=highest, preferred_element_type=jnp.float32,
            )
            pair_t = lax.dot_general(
                own_in, own_grad, (((1,), (1,)), ((), ())), precision=highest,
                preferred_element_type=jnp.float32,
            )
            acc_ref[first:first + piece, first:] += pair_t * decay_t


def block_terms(cumul, scores_t, scaled_in, out_grad):
    head_count, tok = cumul.shape
    chan = scaled_in.shape[1]
    lanes = chan // head_count * HEADS_PER_STEP
    cum_row = cumul.reshape(head_count, 1, tok)
    cum_col = cumul.reshape(head_count, tok, 1)
    return pl.pallas_call(
        block_kernel,
        grid=(head_count // HEADS_PER_STEP,),
        in_specs=[
            pl.BlockSpec((HEADS_PER_STEP, 1, tok), lambda j: (j, 0, 0)),
            pl.BlockSpec((HEADS_PER_STEP, tok, 1), lambda j: (j, 0, 0)),
            pl.BlockSpec((tok, tok), lambda j: (0, 0)),
            pl.BlockSpec((tok, lanes), lambda j: (0, j)),
            pl.BlockSpec((tok, lanes), lambda j: (0, j)),
        ],
        out_specs=[
            pl.BlockSpec((tok, lanes), lambda j: (0, j)),
            pl.BlockSpec((tok, tok), lambda j: (0, 0)),
        ],
        out_shape=[
            jax.ShapeDtypeStruct((tok, chan), jnp.float32),
            jax.ShapeDtypeStruct((tok, tok), jnp.float32),
        ],
    )(cum_row, cum_col, scores_t, scaled_in, out_grad)


def pack_total(total, state_width):
    head_count = total.shape[0]
    rows = jnp.zeros((8, state_width), jnp.float32)
    return lax.dynamic_update_slice(
        rows, jnp.broadcast_to(total[:, None], (head_count, state_width)), (0, 0)
    )


def join(earlier, later, later_total):
    return jnp.exp(later_total)[:, None, None] * earlier + later


def pick(flag, when_true, when_false):
    return jnp.where(flag, when_true, when_false)


def chip_scans(ends, starts, total):
    chips = lax.axis_size("z")
    core = lax.axis_index("core")
    head_count, width, state_width = ends.shape
    rows = head_count * width
    both = ("z", "core")
    swap = [(0, 1), (1, 0)]
    is_fwd = core == 0
    tot_rows = pack_total(total, state_width)
    mine = pick(is_fwd, ends, starts)
    outgoing = jnp.concatenate(
        [pick(is_fwd, starts, ends).reshape(rows, state_width), tot_rows], axis=0
    )
    incoming = lax.ppermute(outgoing, "core", swap)
    partner = incoming[:rows].reshape(head_count, width, state_width)
    partner_t = incoming[rows:rows + head_count, 0]
    chip_state = join(mine, partner, partner_t)
    chip_t = total + partner_t

    def packed(state, tot):
        return jnp.concatenate(
            [state.reshape(rows, state_width), pack_total(tot, state_width)], axis=0
        )

    def unpacked(value):
        return value[:rows].reshape(head_count, width, state_width), value[rows:rows + head_count, 0]

    def move(value, hop):
        pairs = []
        for z in range(chips):
            if z + hop < chips:
                pairs.append((2 * z, 2 * (z + hop)))
            if z - hop >= 0:
                pairs.append((2 * z + 1, 2 * (z - hop) + 1))
        return lax.ppermute(value, both, pairs)

    running = move(packed(chip_state, chip_t), 1)
    hop = 1
    while hop < chips:
        got_state, got_t = unpacked(move(running, hop))
        run_state, run_t = unpacked(running)
        running = packed(join(got_state, run_state, run_t), got_t + run_t)
        hop *= 2
    prefix, unused = unpacked(running)
    joined = join(prefix, mine, total)
    back = lax.ppermute(joined.reshape(rows, state_width), "core", swap)
    other = back.reshape(head_count, width, state_width)
    state_in = pick(is_fwd, prefix, other)
    state_grad = pick(is_fwd, other, prefix)
    return state_in, state_grad


def per_device(
    head_inputs, input_proj, output_mapping, decay_codes, boundary, head_decay_speeds, out_grad
):
    tok_count = head_inputs.shape[0]
    head_count = decay_codes.shape[0]
    head_width = head_inputs.shape[1] // head_count
    state_width = input_proj.shape[1]
    increment_length = step_table(decay_codes)
    logarithm_decay = (
        -head_decay_speeds[:, None] * increment_length
        - sudden_falloff * boundary.astype(jnp.float32)[None, :]
    )
    cumul = jnp.cumsum(logarithm_decay, axis=1)
    group_total = cumul[:, -1]
    to_end = spread_heads(jnp.exp(group_total[:, None] - cumul), head_width)
    from_start = spread_heads(jnp.exp(cumul), head_width)
    scaled_in = head_inputs * spread_heads(increment_length, head_width)
    weighted_in = scaled_in * to_end
    weighted_grad = out_grad * from_start
    ends = jnp.einsum("tk,tn->kn", weighted_in, input_proj, precision=highest)
    starts = jnp.einsum("tk,tn->kn", weighted_grad, output_mapping, precision=highest)
    state_in, state_grad = chip_scans(
        ends.reshape(head_count, head_width, state_width),
        starts.reshape(head_count, head_width, state_width),
        group_total,
    )

    scores_t = jnp.einsum("sn,tn->st", input_proj, output_mapping, precision=highest)
    grad_scaled, grad_scores_t = block_terms(cumul, scores_t, scaled_in, out_grad)
    block_b = jnp.dot(grad_scores_t, output_mapping, precision=highest)
    block_c = jnp.einsum("st,sn->tn", grad_scores_t, input_proj, precision=highest)

    flat_in = state_in.reshape(head_count * head_width, state_width)
    flat_grad = state_grad.reshape(head_count * head_width, state_width)
    carry_c = jnp.dot(weighted_grad, flat_in, precision=highest)
    carry_b = jnp.dot(weighted_in, flat_grad, precision=highest)
    carry_x = to_end * jnp.einsum("tn,kn->tk", input_proj, flat_grad, precision=highest)
    grad_inputs = (grad_scaled + carry_x) * spread_heads(increment_length, head_width)

    both = jnp.concatenate([block_b + carry_b, block_c + carry_c], axis=1)
    parts = lax.axis_size("head")
    spread = lax.all_to_all(both, "head", 0, 0, tiled=True)
    summed = spread.reshape(parts, tok_count // parts, 2 * state_width).sum(axis=0)
    return (grad_inputs, summed[:, :state_width], summed[:, state_width:])


def solution(mesh):
    seq_count, head_parts = mesh.devices.shape
    split = jax.sharding.Mesh(
        mesh.devices.reshape(seq_count // 2, 2, head_parts), ("z", "core", "head")
    )
    seq = ("z", "core")
    return jax.shard_map(
        per_device,
        mesh=split,
        in_specs=(
            P(seq, "head"),
            P(seq, None),
            P(seq, None),
            P("head", seq),
            P(seq),
            P("head"),
            P(seq, "head"),
        ),
        out_specs=(P(seq, "head"), P(("z", "core", "head"), None), P(("z", "core", "head"), None)),
        check_vma=False,
    )
```

```python
import jax
import jax.numpy as jnp
from jax import lax
from jax.experimental import pallas as pl
from jax.experimental.pallas import tpu as pltpu
from jax.sharding import PartitionSpec as P

sudden_falloff = 0.35
highest = lax.Precision.HIGHEST
HEADS_PER_STEP = 2


def step_table(decay_codes):
    levels = jnp.arange(16, dtype=jnp.int32)
    values = 0.5 * 4.0 ** (levels.astype(jnp.float32) / 15.0)
    matching_label = decay_codes[None, :, :] == levels[:, None, None]
    return jnp.sum(jnp.where(matching_label, values[:, None, None], 0.0), axis=0)


def spread_heads(per_head, head_width):
    head_count, tok_count = per_head.shape
    wide = jnp.broadcast_to(per_head.T[:, :, None], (tok_count, head_count, head_width))
    return wide.reshape(tok_count, head_count * head_width)


def block_kernel(cum_ref, cum_t_ref, proj_in_ref, proj_out_ref, in_ref, grad_ref, flow_ref, acc_ref,
                 scores_t_ref):
    step = pl.program_id(0)

    @pl.when(step == 0)
    def _():
        acc_ref[...] = jnp.zeros_like(acc_ref)
        scores_t_ref[...] = lax.dot_general(
            proj_in_ref[...], proj_out_ref[...], (((1,), (1,)), ((), ())), precision=highest,
            preferred_element_type=jnp.float32,
        )

    tok = scores_t_ref.shape[0]
    width = in_ref.shape[1] // HEADS_PER_STEP
    head_count = cum_ref.shape[0]
    piece = 128
    which = lax.broadcasted_iota(jnp.int32, (tok, head_count), 1)
    for k in range(HEADS_PER_STEP):
        head = step * HEADS_PER_STEP + k
        cum_row = cum_ref[pl.ds(head, 1), :]
        cum_col = jnp.sum(jnp.where(which == head, cum_t_ref[...], 0.0), axis=1, keepdims=True)
        lanes = slice(k * width, (k + 1) * width)
        for first in range(0, tok, piece):
            span = tok - first
            rows = lax.broadcasted_iota(jnp.int32, (piece, span), 0)
            cols = lax.broadcasted_iota(jnp.int32, (piece, span), 1)
            later = cols >= rows
            gap = cum_row[:, first:] - cum_col[first:first + piece, :]
            decay_t = jnp.where(later, jnp.exp(jnp.where(later, gap, 0.0)), 0.0)
            own_in = in_ref[first:first + piece, lanes]
            own_grad = grad_ref[first:, lanes]
            flow_ref[first:first + piece, lanes] = jnp.dot(
                scores_t_ref[first:first + piece, first:] * decay_t, own_grad,
                precision=highest, preferred_element_type=jnp.float32,
            )
            pair_t = lax.dot_general(
                own_in, own_grad, (((1,), (1,)), ((), ())), precision=highest,
                preferred_element_type=jnp.float32,
            )
            acc_ref[first:first + piece, first:] += pair_t * decay_t


def block_terms(cumul, input_proj, output_mapping, scaled_in, out_grad):
    head_count, tok = cumul.shape
    chan = scaled_in.shape[1]
    state_width = input_proj.shape[1]
    lanes = chan // head_count * HEADS_PER_STEP
    return pl.pallas_call(
        block_kernel,
        grid=(head_count // HEADS_PER_STEP,),
        in_specs=[
            pl.BlockSpec((head_count, tok), lambda j: (0, 0)),
            pl.BlockSpec((tok, head_count), lambda j: (0, 0)),
            pl.BlockSpec((tok, state_width), lambda j: (0, 0)),
            pl.BlockSpec((tok, state_width), lambda j: (0, 0)),
            pl.BlockSpec((tok, lanes), lambda j: (0, j)),
            pl.BlockSpec((tok, lanes), lambda j: (0, j)),
        ],
        out_specs=[
            pl.BlockSpec((tok, lanes), lambda j: (0, j)),
            pl.BlockSpec((tok, tok), lambda j: (0, 0)),
        ],
        out_shape=[
            jax.ShapeDtypeStruct((tok, chan), jnp.float32),
            jax.ShapeDtypeStruct((tok, tok), jnp.float32),
        ],
        scratch_shapes=[pltpu.VMEM((tok, tok), jnp.float32)],
    )(cumul, cumul.T, input_proj, output_mapping, scaled_in, out_grad)


def pack_total(total, state_width):
    head_count = total.shape[0]
    rows = jnp.zeros((8, state_width), jnp.float32)
    return lax.dynamic_update_slice(
        rows, jnp.broadcast_to(total[:, None], (head_count, state_width)), (0, 0)
    )


def join(earlier, later, later_total):
    return jnp.exp(later_total)[:, None, None] * earlier + later


def pick(flag, when_true, when_false):
    return jnp.where(flag, when_true, when_false)


def chip_scans(ends, starts, total):
    chips = lax.axis_size("z")
    core = lax.axis_index("core")
    head_count, width, state_width = ends.shape
    rows = head_count * width
    both = ("z", "core")
    swap = [(0, 1), (1, 0)]
    is_fwd = core == 0
    tot_rows = pack_total(total, state_width)
    mine = pick(is_fwd, ends, starts)
    outgoing = jnp.concatenate(
        [pick(is_fwd, starts, ends).reshape(rows, state_width), tot_rows], axis=0
    )
    incoming = lax.ppermute(outgoing, "core", swap)
    partner = incoming[:rows].reshape(head_count, width, state_width)
    partner_t = incoming[rows:rows + head_count, 0]
    chip_state = join(mine, partner, partner_t)
    chip_t = total + partner_t

    def packed(state, tot):
        return jnp.concatenate(
            [state.reshape(rows, state_width), pack_total(tot, state_width)], axis=0
        )

    def unpacked(value):
        return value[:rows].reshape(head_count, width, state_width), value[rows:rows + head_count, 0]

    def move(value, hop):
        pairs = []
        for z in range(chips):
            if z + hop < chips:
                pairs.append((2 * z, 2 * (z + hop)))
            if z - hop >= 0:
                pairs.append((2 * z + 1, 2 * (z - hop) + 1))
        return lax.ppermute(value, both, pairs)

    running = move(packed(chip_state, chip_t), 1)
    hop = 1
    while hop < chips:
        got_state, got_t = unpacked(move(running, hop))
        run_state, run_t = unpacked(running)
        running = packed(join(got_state, run_state, run_t), got_t + run_t)
        hop *= 2
    prefix, unused = unpacked(running)
    joined = join(prefix, mine, total)
    back = lax.ppermute(joined.reshape(rows, state_width), "core", swap)
    other = back.reshape(head_count, width, state_width)
    state_in = pick(is_fwd, prefix, other)
    state_grad = pick(is_fwd, other, prefix)
    return state_in, state_grad


def per_device(
    head_inputs, input_proj, output_mapping, decay_codes, boundary, head_decay_speeds, out_grad
):
    tok_count = head_inputs.shape[0]
    head_count = decay_codes.shape[0]
    head_width = head_inputs.shape[1] // head_count
    state_width = input_proj.shape[1]
    increment_length = step_table(decay_codes)
    logarithm_decay = (
        -head_decay_speeds[:, None] * increment_length
        - sudden_falloff * boundary.astype(jnp.float32)[None, :]
    )
    cumul = jnp.cumsum(logarithm_decay, axis=1)
    group_total = cumul[:, -1]
    to_end = spread_heads(jnp.exp(group_total[:, None] - cumul), head_width)
    from_start = spread_heads(jnp.exp(cumul), head_width)
    scaled_in = head_inputs * spread_heads(increment_length, head_width)
    weighted_in = scaled_in * to_end
    weighted_grad = out_grad * from_start
    ends = jnp.einsum("tk,tn->kn", weighted_in, input_proj, precision=highest)
    starts = jnp.einsum("tk,tn->kn", weighted_grad, output_mapping, precision=highest)
    state_in, state_grad = chip_scans(
        ends.reshape(head_count, head_width, state_width),
        starts.reshape(head_count, head_width, state_width),
        group_total,
    )

    grad_scaled, grad_scores_t = block_terms(cumul, input_proj, output_mapping, scaled_in, out_grad)
    block_b = jnp.dot(grad_scores_t, output_mapping, precision=highest)
    block_c = jnp.einsum("st,sn->tn", grad_scores_t, input_proj, precision=highest)

    flat_in = state_in.reshape(head_count * head_width, state_width)
    flat_grad = state_grad.reshape(head_count * head_width, state_width)
    carry_c = jnp.dot(weighted_grad, flat_in, precision=highest)
    carry_b = jnp.dot(weighted_in, flat_grad, precision=highest)
    carry_x = to_end * jnp.einsum("tn,kn->tk", input_proj, flat_grad, precision=highest)
    grad_inputs = (grad_scaled + carry_x) * spread_heads(increment_length, head_width)

    both = jnp.concatenate([block_b + carry_b, block_c + carry_c], axis=1)
    parts = lax.axis_size("head")
    spread = lax.all_to_all(both, "head", 0, 0, tiled=True)
    summed = spread.reshape(parts, tok_count // parts, 2 * state_width).sum(axis=0)
    return (grad_inputs, summed[:, :state_width], summed[:, state_width:])


def solution(mesh):
    seq_count, head_parts = mesh.devices.shape
    split = jax.sharding.Mesh(
        mesh.devices.reshape(seq_count // 2, 2, head_parts), ("z", "core", "head")
    )
    seq = ("z", "core")
    return jax.shard_map(
        per_device,
        mesh=split,
        in_specs=(
            P(seq, "head"),
            P(seq, None),
            P(seq, None),
            P("head", seq),
            P(seq),
            P("head"),
            P(seq, "head"),
        ),
        out_specs=(P(seq, "head"), P(("z", "core", "head"), None), P(("z", "core", "head"), None)),
        check_vma=False,
    )
```

```python
import jax
import jax.numpy as jnp
from jax import lax
from jax.experimental import pallas as pl
from jax.experimental.pallas import tpu as pltpu
from jax.sharding import PartitionSpec as P

sudden_falloff = 0.35
highest = lax.Precision.HIGHEST
HEADS_PER_STEP = 2


def step_table(decay_codes):
    levels = jnp.arange(16, dtype=jnp.int32)
    values = 0.5 * 4.0 ** (levels.astype(jnp.float32) / 15.0)
    matching_label = decay_codes[None, :, :] == levels[:, None, None]
    return jnp.sum(jnp.where(matching_label, values[:, None, None], 0.0), axis=0)


def spread_heads(per_head, head_width):
    head_count, tok_count = per_head.shape
    wide = jnp.broadcast_to(per_head.T[:, :, None], (tok_count, head_count, head_width))
    return wide.reshape(tok_count, head_count * head_width)


def block_kernel(cum_ref, cum_t_ref, proj_in_ref, proj_out_ref, in_ref, grad_ref, flow_ref, part_b_ref,
                 part_c_ref, acc_ref, scores_t_ref):
    step = pl.program_id(0)

    @pl.when(step == 0)
    def _():
        acc_ref[...] = jnp.zeros_like(acc_ref)
        scores_t_ref[...] = lax.dot_general(
            proj_in_ref[...], proj_out_ref[...], (((1,), (1,)), ((), ())), precision=highest,
            preferred_element_type=jnp.float32,
        )

    tok = scores_t_ref.shape[0]
    width = in_ref.shape[1] // HEADS_PER_STEP
    head_count = cum_ref.shape[0]
    piece = 128
    which = lax.broadcasted_iota(jnp.int32, (tok, head_count), 1)
    for k in range(HEADS_PER_STEP):
        head = step * HEADS_PER_STEP + k
        cum_row = cum_ref[pl.ds(head, 1), :]
        cum_col = jnp.sum(jnp.where(which == head, cum_t_ref[...], 0.0), axis=1, keepdims=True)
        lanes = slice(k * width, (k + 1) * width)
        for first in range(0, tok, piece):
            span = tok - first
            rows = lax.broadcasted_iota(jnp.int32, (piece, span), 0)
            cols = lax.broadcasted_iota(jnp.int32, (piece, span), 1)
            later = cols >= rows
            gap = cum_row[:, first:] - cum_col[first:first + piece, :]
            decay_t = jnp.where(later, jnp.exp(jnp.where(later, gap, 0.0)), 0.0)
            own_in = in_ref[first:first + piece, lanes]
            own_grad = grad_ref[first:, lanes]
            flow_ref[first:first + piece, lanes] = jnp.dot(
                scores_t_ref[first:first + piece, first:] * decay_t, own_grad,
                precision=highest, preferred_element_type=jnp.float32,
            )
            pair_t = lax.dot_general(
                own_in, own_grad, (((1,), (1,)), ((), ())), precision=highest,
                preferred_element_type=jnp.float32,
            )
            acc_ref[first:first + piece, first:] += pair_t * decay_t

    @pl.when(step == pl.num_programs(0) - 1)
    def _():
        acc = acc_ref[...]
        part_b_ref[...] = jnp.dot(
            acc, proj_out_ref[...], precision=highest, preferred_element_type=jnp.float32
        )
        part_c_ref[...] = jnp.dot(
            jnp.transpose(acc), proj_in_ref[...], precision=highest,
            preferred_element_type=jnp.float32,
        )


def block_terms(cumul, input_proj, output_mapping, scaled_in, out_grad):
    head_count, tok = cumul.shape
    chan = scaled_in.shape[1]
    state_width = input_proj.shape[1]
    lanes = chan // head_count * HEADS_PER_STEP
    return pl.pallas_call(
        block_kernel,
        grid=(head_count // HEADS_PER_STEP,),
        in_specs=[
            pl.BlockSpec((head_count, tok), lambda j: (0, 0)),
            pl.BlockSpec((tok, head_count), lambda j: (0, 0)),
            pl.BlockSpec((tok, state_width), lambda j: (0, 0)),
            pl.BlockSpec((tok, state_width), lambda j: (0, 0)),
            pl.BlockSpec((tok, lanes), lambda j: (0, j)),
            pl.BlockSpec((tok, lanes), lambda j: (0, j)),
        ],
        out_specs=[
            pl.BlockSpec((tok, lanes), lambda j: (0, j)),
            pl.BlockSpec((tok, state_width), lambda j: (0, 0)),
            pl.BlockSpec((tok, state_width), lambda j: (0, 0)),
        ],
        out_shape=[
            jax.ShapeDtypeStruct((tok, chan), jnp.float32),
            jax.ShapeDtypeStruct((tok, state_width), jnp.float32),
            jax.ShapeDtypeStruct((tok, state_width), jnp.float32),
        ],
        scratch_shapes=[pltpu.VMEM((tok, tok), jnp.float32), pltpu.VMEM((tok, tok), jnp.float32)],
    )(cumul, cumul.T, input_proj, output_mapping, scaled_in, out_grad)


def pack_total(total, state_width):
    head_count = total.shape[0]
    rows = jnp.zeros((8, state_width), jnp.float32)
    return lax.dynamic_update_slice(
        rows, jnp.broadcast_to(total[:, None], (head_count, state_width)), (0, 0)
    )


def join(earlier, later, later_total):
    return jnp.exp(later_total)[:, None, None] * earlier + later


def pick(flag, when_true, when_false):
    return jnp.where(flag, when_true, when_false)


def chip_scans(ends, starts, total):
    chips = lax.axis_size("z")
    core = lax.axis_index("core")
    head_count, width, state_width = ends.shape
    rows = head_count * width
    both = ("z", "core")
    swap = [(0, 1), (1, 0)]
    is_fwd = core == 0
    tot_rows = pack_total(total, state_width)
    mine = pick(is_fwd, ends, starts)
    outgoing = jnp.concatenate(
        [pick(is_fwd, starts, ends).reshape(rows, state_width), tot_rows], axis=0
    )
    incoming = lax.ppermute(outgoing, "core", swap)
    partner = incoming[:rows].reshape(head_count, width, state_width)
    partner_t = incoming[rows:rows + head_count, 0]
    chip_state = join(mine, partner, partner_t)
    chip_t = total + partner_t

    def packed(state, tot):
        return jnp.concatenate(
            [state.reshape(rows, state_width), pack_total(tot, state_width)], axis=0
        )

    def unpacked(value):
        return value[:rows].reshape(head_count, width, state_width), value[rows:rows + head_count, 0]

    def move(value, hop):
        pairs = []
        for z in range(chips):
            if z + hop < chips:
                pairs.append((2 * z, 2 * (z + hop)))
            if z - hop >= 0:
                pairs.append((2 * z + 1, 2 * (z - hop) + 1))
        return lax.ppermute(value, both, pairs)

    running = move(packed(chip_state, chip_t), 1)
    hop = 1
    while hop < chips:
        got_state, got_t = unpacked(move(running, hop))
        run_state, run_t = unpacked(running)
        running = packed(join(got_state, run_state, run_t), got_t + run_t)
        hop *= 2
    prefix, unused = unpacked(running)
    joined = join(prefix, mine, total)
    back = lax.ppermute(joined.reshape(rows, state_width), "core", swap)
    other = back.reshape(head_count, width, state_width)
    state_in = pick(is_fwd, prefix, other)
    state_grad = pick(is_fwd, other, prefix)
    return state_in, state_grad


def per_device(
    head_inputs, input_proj, output_mapping, decay_codes, boundary, head_decay_speeds, out_grad
):
    tok_count = head_inputs.shape[0]
    head_count = decay_codes.shape[0]
    head_width = head_inputs.shape[1] // head_count
    state_width = input_proj.shape[1]
    increment_length = step_table(decay_codes)
    logarithm_decay = (
        -head_decay_speeds[:, None] * increment_length
        - sudden_falloff * boundary.astype(jnp.float32)[None, :]
    )
    cumul = jnp.cumsum(logarithm_decay, axis=1)
    group_total = cumul[:, -1]
    to_end = spread_heads(jnp.exp(group_total[:, None] - cumul), head_width)
    from_start = spread_heads(jnp.exp(cumul), head_width)
    scaled_in = head_inputs * spread_heads(increment_length, head_width)
    weighted_in = scaled_in * to_end
    weighted_grad = out_grad * from_start
    ends = jnp.einsum("tk,tn->kn", weighted_in, input_proj, precision=highest)
    starts = jnp.einsum("tk,tn->kn", weighted_grad, output_mapping, precision=highest)
    state_in, state_grad = chip_scans(
        ends.reshape(head_count, head_width, state_width),
        starts.reshape(head_count, head_width, state_width),
        group_total,
    )

    grad_scaled, block_b, block_c = block_terms(
        cumul, input_proj, output_mapping, scaled_in, out_grad
    )

    flat_in = state_in.reshape(head_count * head_width, state_width)
    flat_grad = state_grad.reshape(head_count * head_width, state_width)
    carry_c = jnp.dot(weighted_grad, flat_in, precision=highest)
    carry_b = jnp.dot(weighted_in, flat_grad, precision=highest)
    carry_x = to_end * jnp.einsum("tn,kn->tk", input_proj, flat_grad, precision=highest)
    grad_inputs = (grad_scaled + carry_x) * spread_heads(increment_length, head_width)

    both = jnp.concatenate([block_b + carry_b, block_c + carry_c], axis=1)
    parts = lax.axis_size("head")
    spread = lax.all_to_all(both, "head", 0, 0, tiled=True)
    summed = spread.reshape(parts, tok_count // parts, 2 * state_width).sum(axis=0)
    return (grad_inputs, summed[:, :state_width], summed[:, state_width:])


def solution(mesh):
    seq_count, head_parts = mesh.devices.shape
    split = jax.sharding.Mesh(
        mesh.devices.reshape(seq_count // 2, 2, head_parts), ("z", "core", "head")
    )
    seq = ("z", "core")
    return jax.shard_map(
        per_device,
        mesh=split,
        in_specs=(
            P(seq, "head"),
            P(seq, None),
            P(seq, None),
            P("head", seq),
            P(seq),
            P("head"),
            P(seq, "head"),
        ),
        out_specs=(P(seq, "head"), P(("z", "core", "head"), None), P(("z", "core", "head"), None)),
        check_vma=False,
    )
```

```python
import jax
import jax.numpy as jnp
from jax import lax
from jax.experimental import pallas as pl
from jax.experimental.pallas import tpu as pltpu
from jax.sharding import PartitionSpec as P

sudden_falloff = 0.35
highest = lax.Precision.HIGHEST
HEADS_PER_STEP = 4


def step_table(decay_codes):
    levels = jnp.arange(16, dtype=jnp.int32)
    values = 0.5 * 4.0 ** (levels.astype(jnp.float32) / 15.0)
    matching_label = decay_codes[None, :, :] == levels[:, None, None]
    return jnp.sum(jnp.where(matching_label, values[:, None, None], 0.0), axis=0)


def spread_heads(per_head, head_width):
    head_count, tok_count = per_head.shape
    wide = jnp.broadcast_to(per_head.T[:, :, None], (tok_count, head_count, head_width))
    return wide.reshape(tok_count, head_count * head_width)


def block_kernel(cum_ref, cum_t_ref, proj_in_ref, proj_out_ref, in_ref, grad_ref, flow_ref, acc_ref,
                 scores_t_ref):
    step = pl.program_id(0)

    @pl.when(step == 0)
    def _():
        acc_ref[...] = jnp.zeros_like(acc_ref)
        scores_t_ref[...] = lax.dot_general(
            proj_in_ref[...], proj_out_ref[...], (((1,), (1,)), ((), ())), precision=highest,
            preferred_element_type=jnp.float32,
        )

    tok = scores_t_ref.shape[0]
    width = in_ref.shape[1] // HEADS_PER_STEP
    head_count = cum_ref.shape[0]
    piece = 128
    which = lax.broadcasted_iota(jnp.int32, (tok, head_count), 1)
    for k in range(HEADS_PER_STEP):
        head = step * HEADS_PER_STEP + k
        cum_row = cum_ref[pl.ds(head, 1), :]
        cum_col = jnp.sum(jnp.where(which == head, cum_t_ref[...], 0.0), axis=1, keepdims=True)
        lanes = slice(k * width, (k + 1) * width)
        for first in range(0, tok, piece):
            span = tok - first
            rows = lax.broadcasted_iota(jnp.int32, (piece, span), 0)
            cols = lax.broadcasted_iota(jnp.int32, (piece, span), 1)
            later = cols >= rows
            gap = cum_row[:, first:] - cum_col[first:first + piece, :]
            decay_t = jnp.where(later, jnp.exp(gap), 0.0)
            own_in = in_ref[first:first + piece, lanes]
            own_grad = grad_ref[first:, lanes]
            flow_ref[first:first + piece, lanes] = jnp.dot(
                scores_t_ref[first:first + piece, first:] * decay_t, own_grad,
                precision=highest, preferred_element_type=jnp.float32,
            )
            pair_t = lax.dot_general(
                own_in, own_grad, (((1,), (1,)), ((), ())), precision=highest,
                preferred_element_type=jnp.float32,
            )
            acc_ref[first:first + piece, first:] += pair_t * decay_t


def block_terms(cumul, input_proj, output_mapping, scaled_in, out_grad):
    head_count, tok = cumul.shape
    chan = scaled_in.shape[1]
    state_width = input_proj.shape[1]
    lanes = chan // head_count * HEADS_PER_STEP
    return pl.pallas_call(
        block_kernel,
        grid=(head_count // HEADS_PER_STEP,),
        in_specs=[
            pl.BlockSpec((head_count, tok), lambda j: (0, 0)),
            pl.BlockSpec((tok, head_count), lambda j: (0, 0)),
            pl.BlockSpec((tok, state_width), lambda j: (0, 0)),
            pl.BlockSpec((tok, state_width), lambda j: (0, 0)),
            pl.BlockSpec((tok, lanes), lambda j: (0, j)),
            pl.BlockSpec((tok, lanes), lambda j: (0, j)),
        ],
        out_specs=[
            pl.BlockSpec((tok, lanes), lambda j: (0, j)),
            pl.BlockSpec((tok, tok), lambda j: (0, 0)),
        ],
        out_shape=[
            jax.ShapeDtypeStruct((tok, chan), jnp.float32),
            jax.ShapeDtypeStruct((tok, tok), jnp.float32),
        ],
        scratch_shapes=[pltpu.VMEM((tok, tok), jnp.float32)],
    )(cumul, cumul.T, input_proj, output_mapping, scaled_in, out_grad)


def pack_total(total, state_width):
    head_count = total.shape[0]
    rows = jnp.zeros((8, state_width), jnp.float32)
    return lax.dynamic_update_slice(
        rows, jnp.broadcast_to(total[:, None], (head_count, state_width)), (0, 0)
    )


def join(earlier, later, later_total):
    return jnp.exp(later_total)[:, None, None] * earlier + later


def pick(flag, when_true, when_false):
    return jnp.where(flag, when_true, when_false)


def chip_scans(ends, starts, total):
    chips = lax.axis_size("z")
    core = lax.axis_index("core")
    head_count, width, state_width = ends.shape
    rows = head_count * width
    both = ("z", "core")
    swap = [(0, 1), (1, 0)]
    is_fwd = core == 0
    tot_rows = pack_total(total, state_width)
    mine = pick(is_fwd, ends, starts)
    outgoing = jnp.concatenate(
        [pick(is_fwd, starts, ends).reshape(rows, state_width), tot_rows], axis=0
    )
    incoming = lax.ppermute(outgoing, "core", swap)
    partner = incoming[:rows].reshape(head_count, width, state_width)
    partner_t = incoming[rows:rows + head_count, 0]
    chip_state = join(mine, partner, partner_t)
    chip_t = total + partner_t

    def packed(state, tot):
        return jnp.concatenate(
            [state.reshape(rows, state_width), pack_total(tot, state_width)], axis=0
        )

    def unpacked(value):
        return value[:rows].reshape(head_count, width, state_width), value[rows:rows + head_count, 0]

    def move(value, hop):
        pairs = []
        for z in range(chips):
            if z + hop < chips:
                pairs.append((2 * z, 2 * (z + hop)))
            if z - hop >= 0:
                pairs.append((2 * z + 1, 2 * (z - hop) + 1))
        return lax.ppermute(value, both, pairs)

    running = move(packed(chip_state, chip_t), 1)
    hop = 1
    while hop < chips:
        got_state, got_t = unpacked(move(running, hop))
        run_state, run_t = unpacked(running)
        running = packed(join(got_state, run_state, run_t), got_t + run_t)
        hop *= 2
    prefix, unused = unpacked(running)
    joined = join(prefix, mine, total)
    back = lax.ppermute(joined.reshape(rows, state_width), "core", swap)
    other = back.reshape(head_count, width, state_width)
    state_in = pick(is_fwd, prefix, other)
    state_grad = pick(is_fwd, other, prefix)
    return state_in, state_grad


def per_device(
    head_inputs, input_proj, output_mapping, decay_codes, boundary, head_decay_speeds, out_grad
):
    tok_count = head_inputs.shape[0]
    head_count = decay_codes.shape[0]
    head_width = head_inputs.shape[1] // head_count
    state_width = input_proj.shape[1]
    increment_length = step_table(decay_codes)
    logarithm_decay = (
        -head_decay_speeds[:, None] * increment_length
        - sudden_falloff * boundary.astype(jnp.float32)[None, :]
    )
    cumul = jnp.cumsum(logarithm_decay, axis=1)
    group_total = cumul[:, -1]
    to_end = spread_heads(jnp.exp(group_total[:, None] - cumul), head_width)
    from_start = spread_heads(jnp.exp(cumul), head_width)
    scaled_in = head_inputs * spread_heads(increment_length, head_width)
    weighted_in = scaled_in * to_end
    weighted_grad = out_grad * from_start
    ends = jnp.einsum("tk,tn->kn", weighted_in, input_proj, precision=highest)
    starts = jnp.einsum("tk,tn->kn", weighted_grad, output_mapping, precision=highest)
    state_in, state_grad = chip_scans(
        ends.reshape(head_count, head_width, state_width),
        starts.reshape(head_count, head_width, state_width),
        group_total,
    )

    grad_scaled, grad_scores_t = block_terms(cumul, input_proj, output_mapping, scaled_in, out_grad)
    block_b = jnp.dot(grad_scores_t, output_mapping, precision=highest)
    block_c = jnp.einsum("st,sn->tn", grad_scores_t, input_proj, precision=highest)

    flat_in = state_in.reshape(head_count * head_width, state_width)
    flat_grad = state_grad.reshape(head_count * head_width, state_width)
    carry_c = jnp.dot(weighted_grad, flat_in, precision=highest)
    carry_b = jnp.dot(weighted_in, flat_grad, precision=highest)
    carry_x = to_end * jnp.einsum("tn,kn->tk", input_proj, flat_grad, precision=highest)
    grad_inputs = (grad_scaled + carry_x) * spread_heads(increment_length, head_width)

    both = jnp.concatenate([block_b + carry_b, block_c + carry_c], axis=1)
    parts = lax.axis_size("head")
    spread = lax.all_to_all(both, "head", 0, 0, tiled=True)
    summed = spread.reshape(parts, tok_count // parts, 2 * state_width).sum(axis=0)
    return (grad_inputs, summed[:, :state_width], summed[:, state_width:])


def solution(mesh):
    seq_count, head_parts = mesh.devices.shape
    split = jax.sharding.Mesh(
        mesh.devices.reshape(seq_count // 2, 2, head_parts), ("z", "core", "head")
    )
    seq = ("z", "core")
    return jax.shard_map(
        per_device,
        mesh=split,
        in_specs=(
            P(seq, "head"),
            P(seq, None),
            P(seq, None),
            P("head", seq),
            P(seq),
            P("head"),
            P(seq, "head"),
        ),
        out_specs=(P(seq, "head"), P(("z", "core", "head"), None), P(("z", "core", "head"), None)),
        check_vma=False,
    )
```

```python
import jax
import jax.numpy as jnp
from jax import lax
from jax.experimental import pallas as pl
from jax.experimental.pallas import tpu as pltpu
from jax.sharding import PartitionSpec as P

sudden_falloff = 0.35
highest = lax.Precision.HIGHEST
HEADS_PER_STEP = 4


def step_table(decay_codes):
    levels = jnp.arange(16, dtype=jnp.int32)
    values = 0.5 * 4.0 ** (levels.astype(jnp.float32) / 15.0)
    matching_label = decay_codes[None, :, :] == levels[:, None, None]
    return jnp.sum(jnp.where(matching_label, values[:, None, None], 0.0), axis=0)


def spread_heads(per_head, head_width):
    head_count, tok_count = per_head.shape
    wide = jnp.broadcast_to(per_head.T[:, :, None], (tok_count, head_count, head_width))
    return wide.reshape(tok_count, head_count * head_width)


def block_kernel(cum_ref, cum_t_ref, proj_in_ref, proj_out_ref, in_ref, grad_ref, flow_ref, acc_ref,
                 scores_t_ref):
    step = pl.program_id(0)

    @pl.when(step == 0)
    def _():
        acc_ref[...] = jnp.zeros_like(acc_ref)
        scores_t_ref[...] = lax.dot_general(
            proj_in_ref[...], proj_out_ref[...], (((1,), (1,)), ((), ())), precision=highest,
            preferred_element_type=jnp.float32,
        )

    tok = scores_t_ref.shape[0]
    width = in_ref.shape[1] // HEADS_PER_STEP
    head_count = cum_ref.shape[0]
    piece = 128
    which = lax.broadcasted_iota(jnp.int32, (tok, head_count), 1)
    for k in range(HEADS_PER_STEP):
        head = step * HEADS_PER_STEP + k
        cum_row = cum_ref[pl.ds(head, 1), :]
        cum_col = jnp.sum(jnp.where(which == head, cum_t_ref[...], 0.0), axis=1, keepdims=True)
        lanes = slice(k * width, (k + 1) * width)
        for first in range(0, tok, piece):
            span = tok - first
            rows = lax.broadcasted_iota(jnp.int32, (piece, span), 0)
            cols = lax.broadcasted_iota(jnp.int32, (piece, span), 1)
            later = cols >= rows
            gap = cum_row[:, first:] - cum_col[first:first + piece, :]
            decay_t = jnp.where(later, jnp.exp(gap), 0.0)
            own_in = in_ref[first:first + piece, lanes]
            own_grad = grad_ref[first:, lanes]
            flow_ref[first:first + piece, lanes] = jnp.dot(
                scores_t_ref[first:first + piece, first:] * decay_t, own_grad,
                precision=highest, preferred_element_type=jnp.float32,
            )
            pair_t = lax.dot_general(
                own_in, own_grad, (((1,), (1,)), ((), ())), precision=highest,
                preferred_element_type=jnp.float32,
            )
            acc_ref[first:first + piece, first:] += pair_t * decay_t


def block_terms(cumul, input_proj, output_mapping, scaled_in, out_grad):
    head_count, tok = cumul.shape
    chan = scaled_in.shape[1]
    state_width = input_proj.shape[1]
    lanes = chan // head_count * HEADS_PER_STEP
    return pl.pallas_call(
        block_kernel,
        grid=(head_count // HEADS_PER_STEP,),
        in_specs=[
            pl.BlockSpec((head_count, tok), lambda j: (0, 0)),
            pl.BlockSpec((tok, head_count), lambda j: (0, 0)),
            pl.BlockSpec((tok, state_width), lambda j: (0, 0)),
            pl.BlockSpec((tok, state_width), lambda j: (0, 0)),
            pl.BlockSpec((tok, lanes), lambda j: (0, j)),
            pl.BlockSpec((tok, lanes), lambda j: (0, j)),
        ],
        out_specs=[
            pl.BlockSpec((tok, lanes), lambda j: (0, j)),
            pl.BlockSpec((tok, tok), lambda j: (0, 0)),
        ],
        out_shape=[
            jax.ShapeDtypeStruct((tok, chan), jnp.float32),
            jax.ShapeDtypeStruct((tok, tok), jnp.float32),
        ],
        scratch_shapes=[pltpu.VMEM((tok, tok), jnp.float32)],
    )(cumul, cumul.T, input_proj, output_mapping, scaled_in, out_grad)


def pack_total(total, state_width):
    head_count = total.shape[0]
    rows = jnp.zeros((8, state_width), jnp.float32)
    return lax.dynamic_update_slice(
        rows, jnp.broadcast_to(total[:, None], (head_count, state_width)), (0, 0)
    )


def join(earlier, later, later_total):
    return jnp.exp(later_total)[:, None, None] * earlier + later


def pick(flag, when_true, when_false):
    return jnp.where(flag, when_true, when_false)


def chip_scans(ends, starts, total):
    chips = lax.axis_size("z")
    core = lax.axis_index("core")
    head_count, width, state_width = ends.shape
    rows = head_count * width
    both = ("z", "core")
    swap = [(0, 1), (1, 0)]
    is_fwd = core == 0
    mine = pick(is_fwd, ends, starts)
    other = pick(is_fwd, starts, ends)

    def packed(state, tot):
        return jnp.concatenate(
            [state.reshape(rows, state_width), pack_total(tot, state_width)], axis=0
        )

    def unpacked(value):
        return value[:rows].reshape(head_count, width, state_width), value[rows:rows + head_count, 0]

    def move(value, hop):
        pairs = []
        for z in range(chips):
            if z + hop < chips:
                pairs.append((2 * z, 2 * (z + hop)))
            if z - hop >= 0:
                pairs.append((2 * z + 1, 2 * (z - hop) + 1))
        return lax.ppermute(value, both, pairs)

    cross = []
    for z in range(chips):
        if z + 1 < chips:
            cross.append((2 * z + 1, 2 * (z + 1)))
        if z - 1 >= 0:
            cross.append((2 * z, 2 * (z - 1) + 1))
    near_state, near_t = unpacked(move(packed(mine, total), 1))
    far_state, far_t = unpacked(lax.ppermute(packed(other, total), both, cross))
    running = packed(join(near_state, far_state, far_t), near_t + far_t)
    hop = 1
    while hop < chips:
        got_state, got_t = unpacked(move(running, hop))
        run_state, run_t = unpacked(running)
        running = packed(join(got_state, run_state, run_t), got_t + run_t)
        hop *= 2
    prefix, unused = unpacked(running)
    joined = join(prefix, mine, total)
    back = lax.ppermute(joined.reshape(rows, state_width), "core", swap)
    other = back.reshape(head_count, width, state_width)
    state_in = pick(is_fwd, prefix, other)
    state_grad = pick(is_fwd, other, prefix)
    return state_in, state_grad


def per_device(
    head_inputs, input_proj, output_mapping, decay_codes, boundary, head_decay_speeds, out_grad
):
    tok_count = head_inputs.shape[0]
    head_count = decay_codes.shape[0]
    head_width = head_inputs.shape[1] // head_count
    state_width = input_proj.shape[1]
    increment_length = step_table(decay_codes)
    logarithm_decay = (
        -head_decay_speeds[:, None] * increment_length
        - sudden_falloff * boundary.astype(jnp.float32)[None, :]
    )
    cumul = jnp.cumsum(logarithm_decay, axis=1)
    group_total = cumul[:, -1]
    to_end = spread_heads(jnp.exp(group_total[:, None] - cumul), head_width)
    from_start = spread_heads(jnp.exp(cumul), head_width)
    scaled_in = head_inputs * spread_heads(increment_length, head_width)
    weighted_in = scaled_in * to_end
    weighted_grad = out_grad * from_start
    ends = jnp.einsum("tk,tn->kn", weighted_in, input_proj, precision=highest)
    starts = jnp.einsum("tk,tn->kn", weighted_grad, output_mapping, precision=highest)
    state_in, state_grad = chip_scans(
        ends.reshape(head_count, head_width, state_width),
        starts.reshape(head_count, head_width, state_width),
        group_total,
    )

    grad_scaled, grad_scores_t = block_terms(cumul, input_proj, output_mapping, scaled_in, out_grad)
    block_b = jnp.dot(grad_scores_t, output_mapping, precision=highest)
    block_c = jnp.einsum("st,sn->tn", grad_scores_t, input_proj, precision=highest)

    flat_in = state_in.reshape(head_count * head_width, state_width)
    flat_grad = state_grad.reshape(head_count * head_width, state_width)
    carry_c = jnp.dot(weighted_grad, flat_in, precision=highest)
    carry_b = jnp.dot(weighted_in, flat_grad, precision=highest)
    carry_x = to_end * jnp.einsum("tn,kn->tk", input_proj, flat_grad, precision=highest)
    grad_inputs = (grad_scaled + carry_x) * spread_heads(increment_length, head_width)

    both = jnp.concatenate([block_b + carry_b, block_c + carry_c], axis=1)
    parts = lax.axis_size("head")
    spread = lax.all_to_all(both, "head", 0, 0, tiled=True)
    summed = spread.reshape(parts, tok_count // parts, 2 * state_width).sum(axis=0)
    return (grad_inputs, summed[:, :state_width], summed[:, state_width:])


def solution(mesh):
    seq_count, head_parts = mesh.devices.shape
    split = jax.sharding.Mesh(
        mesh.devices.reshape(seq_count // 2, 2, head_parts), ("z", "core", "head")
    )
    seq = ("z", "core")
    return jax.shard_map(
        per_device,
        mesh=split,
        in_specs=(
            P(seq, "head"),
            P(seq, None),
            P(seq, None),
            P("head", seq),
            P(seq),
            P("head"),
            P(seq, "head"),
        ),
        out_specs=(P(seq, "head"), P(("z", "core", "head"), None), P(("z", "core", "head"), None)),
        check_vma=False,
    )
```

```python
import jax
import jax.numpy as jnp
from jax import lax
from jax.experimental import pallas as pl
from jax.experimental.pallas import tpu as pltpu
from jax.sharding import PartitionSpec as P

sudden_falloff = 0.35
highest = lax.Precision.HIGHEST
HEADS_PER_STEP = 4


def step_table(decay_codes):
    levels = jnp.arange(16, dtype=jnp.int32)
    values = 0.5 * 4.0 ** (levels.astype(jnp.float32) / 15.0)
    matching_label = decay_codes[None, :, :] == levels[:, None, None]
    return jnp.sum(jnp.where(matching_label, values[:, None, None], 0.0), axis=0)


def spread_heads(per_head, head_width):
    head_count, tok_count = per_head.shape
    wide = jnp.broadcast_to(per_head.T[:, :, None], (tok_count, head_count, head_width))
    return wide.reshape(tok_count, head_count * head_width)


def block_kernel(cum_ref, cum_t_ref, proj_in_ref, proj_out_ref, in_ref, grad_ref, flow_ref, acc_ref,
                 scores_t_ref):
    step = pl.program_id(0)

    @pl.when(step == 0)
    def _():
        acc_ref[...] = jnp.zeros_like(acc_ref)
        scores_t_ref[...] = lax.dot_general(
            proj_in_ref[...], proj_out_ref[...], (((1,), (1,)), ((), ())), precision=highest,
            preferred_element_type=jnp.float32,
        )

    tok = scores_t_ref.shape[0]
    width = in_ref.shape[1] // HEADS_PER_STEP
    head_count = cum_ref.shape[0]
    piece = 128
    which = lax.broadcasted_iota(jnp.int32, (tok, head_count), 1)
    for k in range(HEADS_PER_STEP):
        head = step * HEADS_PER_STEP + k
        cum_row = cum_ref[pl.ds(head, 1), :]
        cum_col = jnp.sum(jnp.where(which == head, cum_t_ref[...], 0.0), axis=1, keepdims=True)
        lanes = slice(k * width, (k + 1) * width)
        for first in range(0, tok, piece):
            span = tok - first
            rows = lax.broadcasted_iota(jnp.int32, (piece, span), 0)
            cols = lax.broadcasted_iota(jnp.int32, (piece, span), 1)
            later = cols >= rows
            gap = cum_row[:, first:] - cum_col[first:first + piece, :]
            decay_t = jnp.where(later, jnp.exp(gap), 0.0)
            own_in = in_ref[first:first + piece, lanes]
            own_grad = grad_ref[first:, lanes]
            flow_ref[first:first + piece, lanes] = jnp.dot(
                scores_t_ref[first:first + piece, first:] * decay_t, own_grad,
                precision=highest, preferred_element_type=jnp.float32,
            )
            pair_t = lax.dot_general(
                own_in, own_grad, (((1,), (1,)), ((), ())), precision=highest,
                preferred_element_type=jnp.float32,
            )
            acc_ref[first:first + piece, first:] += pair_t * decay_t


def block_terms(cumul, input_proj, output_mapping, scaled_in, out_grad):
    head_count, tok = cumul.shape
    chan = scaled_in.shape[1]
    state_width = input_proj.shape[1]
    lanes = chan // head_count * HEADS_PER_STEP
    return pl.pallas_call(
        block_kernel,
        grid=(head_count // HEADS_PER_STEP,),
        in_specs=[
            pl.BlockSpec((head_count, tok), lambda j: (0, 0)),
            pl.BlockSpec((tok, head_count), lambda j: (0, 0)),
            pl.BlockSpec((tok, state_width), lambda j: (0, 0)),
            pl.BlockSpec((tok, state_width), lambda j: (0, 0)),
            pl.BlockSpec((tok, lanes), lambda j: (0, j)),
            pl.BlockSpec((tok, lanes), lambda j: (0, j)),
        ],
        out_specs=[
            pl.BlockSpec((tok, lanes), lambda j: (0, j)),
            pl.BlockSpec((tok, tok), lambda j: (0, 0)),
        ],
        out_shape=[
            jax.ShapeDtypeStruct((tok, chan), jnp.float32),
            jax.ShapeDtypeStruct((tok, tok), jnp.float32),
        ],
        scratch_shapes=[pltpu.VMEM((tok, tok), jnp.float32)],
    )(cumul, cumul.T, input_proj, output_mapping, scaled_in, out_grad)


def pack_total(total, state_width):
    head_count = total.shape[0]
    rows = jnp.zeros((8, state_width), jnp.float32)
    return lax.dynamic_update_slice(
        rows, jnp.broadcast_to(total[:, None], (head_count, state_width)), (0, 0)
    )


def join(earlier, later, later_total):
    return jnp.exp(later_total)[:, None, None] * earlier + later


def pick(flag, when_true, when_false):
    return jnp.where(flag, when_true, when_false)


def chip_scans(ends, starts, total):
    chips = lax.axis_size("z")
    core = lax.axis_index("core")
    head_count, width, state_width = ends.shape
    rows = head_count * width
    both = ("z", "core")
    swap = [(0, 1), (1, 0)]
    is_fwd = core == 0
    mine = pick(is_fwd, ends, starts)
    other = pick(is_fwd, starts, ends)

    def packed(state, tot):
        return jnp.concatenate(
            [state.reshape(rows, state_width), pack_total(tot, state_width)], axis=0
        )

    def unpacked(value):
        return value[:rows].reshape(head_count, width, state_width), value[rows:rows + head_count, 0]

    def move(value, hop):
        pairs = []
        for z in range(chips):
            if z + hop < chips:
                pairs.append((2 * z, 2 * (z + hop)))
            if z - hop >= 0:
                pairs.append((2 * z + 1, 2 * (z - hop) + 1))
        return lax.ppermute(value, both, pairs)

    cross = []
    for z in range(chips):
        if z + 1 < chips:
            cross.append((2 * z + 1, 2 * (z + 1)))
        if z - 1 >= 0:
            cross.append((2 * z, 2 * (z - 1) + 1))
    near_state, near_t = unpacked(move(packed(mine, total), 1))
    far_state, far_t = unpacked(lax.ppermute(packed(other, total), both, cross))
    running = packed(join(near_state, far_state, far_t), near_t + far_t)
    hop = 1
    while hop < chips:
        got = move(running, hop)
        run_t = running[rows:rows + head_count, 0]
        scale = jnp.concatenate(
            [jnp.repeat(jnp.exp(run_t), width), jnp.ones((running.shape[0] - rows,), jnp.float32)]
        )
        running = scale[:, None] * got + running
        hop *= 2
    prefix, unused = unpacked(running)
    joined = join(prefix, mine, total)
    back = lax.ppermute(joined.reshape(rows, state_width), "core", swap)
    other = back.reshape(head_count, width, state_width)
    state_in = pick(is_fwd, prefix, other)
    state_grad = pick(is_fwd, other, prefix)
    return state_in, state_grad


def per_device(
    head_inputs, input_proj, output_mapping, decay_codes, boundary, head_decay_speeds, out_grad
):
    tok_count = head_inputs.shape[0]
    head_count = decay_codes.shape[0]
    head_width = head_inputs.shape[1] // head_count
    state_width = input_proj.shape[1]
    increment_length = step_table(decay_codes)
    logarithm_decay = (
        -head_decay_speeds[:, None] * increment_length
        - sudden_falloff * boundary.astype(jnp.float32)[None, :]
    )
    cumul = jnp.cumsum(logarithm_decay, axis=1)
    group_total = cumul[:, -1]
    to_end = spread_heads(jnp.exp(group_total[:, None] - cumul), head_width)
    from_start = spread_heads(jnp.exp(cumul), head_width)
    scaled_in = head_inputs * spread_heads(increment_length, head_width)
    weighted_in = scaled_in * to_end
    weighted_grad = out_grad * from_start
    ends = jnp.einsum("tk,tn->kn", weighted_in, input_proj, precision=highest)
    starts = jnp.einsum("tk,tn->kn", weighted_grad, output_mapping, precision=highest)
    state_in, state_grad = chip_scans(
        ends.reshape(head_count, head_width, state_width),
        starts.reshape(head_count, head_width, state_width),
        group_total,
    )

    grad_scaled, grad_scores_t = block_terms(cumul, input_proj, output_mapping, scaled_in, out_grad)
    block_b = jnp.dot(grad_scores_t, output_mapping, precision=highest)
    block_c = jnp.einsum("st,sn->tn", grad_scores_t, input_proj, precision=highest)

    flat_in = state_in.reshape(head_count * head_width, state_width)
    flat_grad = state_grad.reshape(head_count * head_width, state_width)
    carry_c = jnp.dot(weighted_grad, flat_in, precision=highest)
    carry_b = jnp.dot(weighted_in, flat_grad, precision=highest)
    carry_x = to_end * jnp.einsum("tn,kn->tk", input_proj, flat_grad, precision=highest)
    grad_inputs = (grad_scaled + carry_x) * spread_heads(increment_length, head_width)

    both = jnp.concatenate([block_b + carry_b, block_c + carry_c], axis=1)
    parts = lax.axis_size("head")
    spread = lax.all_to_all(both, "head", 0, 0, tiled=True)
    summed = spread.reshape(parts, tok_count // parts, 2 * state_width).sum(axis=0)
    return (grad_inputs, summed[:, :state_width], summed[:, state_width:])


def solution(mesh):
    seq_count, head_parts = mesh.devices.shape
    split = jax.sharding.Mesh(
        mesh.devices.reshape(seq_count // 2, 2, head_parts), ("z", "core", "head")
    )
    seq = ("z", "core")
    return jax.shard_map(
        per_device,
        mesh=split,
        in_specs=(
            P(seq, "head"),
            P(seq, None),
            P(seq, None),
            P("head", seq),
            P(seq),
            P("head"),
            P(seq, "head"),
        ),
        out_specs=(P(seq, "head"), P(("z", "core", "head"), None), P(("z", "core", "head"), None)),
        check_vma=False,
    )
```

```python
import jax
import jax.numpy as jnp
from jax import lax
from jax.experimental import pallas as pl
from jax.experimental.pallas import tpu as pltpu
from jax.sharding import PartitionSpec as P

sudden_falloff = 0.35
highest = lax.Precision.HIGHEST
HEADS_PER_STEP = 4


def step_table(decay_codes):
    levels = jnp.arange(16, dtype=jnp.int32)
    values = 0.5 * 4.0 ** (levels.astype(jnp.float32) / 15.0)
    matching_label = decay_codes[None, :, :] == levels[:, None, None]
    return jnp.sum(jnp.where(matching_label, values[:, None, None], 0.0), axis=0)


def spread_heads(per_head, head_width):
    head_count, tok_count = per_head.shape
    wide = jnp.broadcast_to(per_head.T[:, :, None], (tok_count, head_count, head_width))
    return wide.reshape(tok_count, head_count * head_width)


def block_kernel(cum_ref, cum_t_ref, proj_in_ref, proj_out_ref, in_ref, grad_ref, flow_ref, acc_ref,
                 scores_t_ref):
    step = pl.program_id(0)

    @pl.when(step == 0)
    def _():
        acc_ref[...] = jnp.zeros_like(acc_ref)
        scores_t_ref[...] = lax.dot_general(
            proj_in_ref[...], proj_out_ref[...], (((1,), (1,)), ((), ())), precision=highest,
            preferred_element_type=jnp.float32,
        )

    tok = scores_t_ref.shape[0]
    width = in_ref.shape[1] // HEADS_PER_STEP
    head_count = cum_ref.shape[0]
    piece = 128
    which = lax.broadcasted_iota(jnp.int32, (tok, head_count), 1)
    for k in range(HEADS_PER_STEP):
        head = step * HEADS_PER_STEP + k
        cum_row = cum_ref[pl.ds(head, 1), :]
        cum_col = jnp.sum(jnp.where(which == head, cum_t_ref[...], 0.0), axis=1, keepdims=True)
        lanes = slice(k * width, (k + 1) * width)
        for first in range(0, tok, piece):
            span = tok - first
            rows = lax.broadcasted_iota(jnp.int32, (piece, span), 0)
            cols = lax.broadcasted_iota(jnp.int32, (piece, span), 1)
            later = cols >= rows
            gap = cum_row[:, first:] - cum_col[first:first + piece, :]
            decay_t = jnp.where(later, jnp.exp(gap), 0.0)
            own_in = in_ref[first:first + piece, lanes]
            own_grad = grad_ref[first:, lanes]
            flow_ref[first:first + piece, lanes] = jnp.dot(
                scores_t_ref[first:first + piece, first:] * decay_t, own_grad,
                precision=highest, preferred_element_type=jnp.float32,
            )
            pair_t = lax.dot_general(
                own_in, own_grad, (((1,), (1,)), ((), ())), precision=highest,
                preferred_element_type=jnp.float32,
            )
            acc_ref[first:first + piece, first:] += pair_t * decay_t


def block_terms(cumul, input_proj, output_mapping, scaled_in, out_grad):
    head_count, tok = cumul.shape
    chan = scaled_in.shape[1]
    state_width = input_proj.shape[1]
    lanes = chan // head_count * HEADS_PER_STEP
    return pl.pallas_call(
        block_kernel,
        grid=(head_count // HEADS_PER_STEP,),
        in_specs=[
            pl.BlockSpec((head_count, tok), lambda j: (0, 0)),
            pl.BlockSpec((tok, head_count), lambda j: (0, 0)),
            pl.BlockSpec((tok, state_width), lambda j: (0, 0)),
            pl.BlockSpec((tok, state_width), lambda j: (0, 0)),
            pl.BlockSpec((tok, lanes), lambda j: (0, j)),
            pl.BlockSpec((tok, lanes), lambda j: (0, j)),
        ],
        out_specs=[
            pl.BlockSpec((tok, lanes), lambda j: (0, j)),
            pl.BlockSpec((tok, tok), lambda j: (0, 0)),
        ],
        out_shape=[
            jax.ShapeDtypeStruct((tok, chan), jnp.float32),
            jax.ShapeDtypeStruct((tok, tok), jnp.float32),
        ],
        scratch_shapes=[pltpu.VMEM((tok, tok), jnp.float32)],
    )(cumul, cumul.T, input_proj, output_mapping, scaled_in, out_grad)


def pack_total(total, state_width):
    head_count = total.shape[0]
    rows = jnp.zeros((8, state_width), jnp.float32)
    return lax.dynamic_update_slice(
        rows, jnp.broadcast_to(total[:, None], (head_count, state_width)), (0, 0)
    )


def join(earlier, later, later_total):
    return jnp.exp(later_total)[:, None, None] * earlier + later


def pick(flag, when_true, when_false):
    return jnp.where(flag, when_true, when_false)


def chip_scans(ends, starts, total):
    chips = lax.axis_size("z")
    core = lax.axis_index("core")
    head_count, width, state_width = ends.shape
    rows = head_count * width
    both = ("z", "core")
    swap = [(0, 1), (1, 0)]
    is_fwd = core == 0
    mine = pick(is_fwd, ends, starts)
    other = pick(is_fwd, starts, ends)

    def packed(state, tot):
        return jnp.concatenate(
            [state.reshape(rows, state_width), pack_total(tot, state_width)], axis=0
        )

    def unpacked(value):
        return value[:rows].reshape(head_count, width, state_width), value[rows:rows + head_count, 0]

    def move(value, hop):
        pairs = []
        for z in range(chips):
            if z + hop < chips:
                pairs.append((2 * z, 2 * (z + hop)))
            if z - hop >= 0:
                pairs.append((2 * z + 1, 2 * (z - hop) + 1))
        return lax.ppermute(value, both, pairs)

    cross = []
    for z in range(chips):
        if z + 1 < chips:
            cross.append((2 * z + 1, 2 * (z + 1)))
        if z - 1 >= 0:
            cross.append((2 * z, 2 * (z - 1) + 1))
    near = move(packed(mine, total), 1)
    far = lax.ppermute(packed(other, total), both, cross)
    far_t = far[rows:rows + head_count, 0]
    first_scale = jnp.concatenate(
        [jnp.repeat(jnp.exp(far_t), width), jnp.ones((far.shape[0] - rows,), jnp.float32)]
    )
    running = first_scale[:, None] * near + far
    hop = 1
    while hop < chips:
        got = move(running, hop)
        run_t = running[rows:rows + head_count, 0]
        scale = jnp.concatenate(
            [jnp.repeat(jnp.exp(run_t), width), jnp.ones((running.shape[0] - rows,), jnp.float32)]
        )
        running = scale[:, None] * got + running
        hop *= 2
    prefix, unused = unpacked(running)
    joined = join(prefix, mine, total)
    back = lax.ppermute(joined.reshape(rows, state_width), "core", swap)
    other = back.reshape(head_count, width, state_width)
    state_in = pick(is_fwd, prefix, other)
    state_grad = pick(is_fwd, other, prefix)
    return state_in, state_grad


def per_device(
    head_inputs, input_proj, output_mapping, decay_codes, boundary, head_decay_speeds, out_grad
):
    tok_count = head_inputs.shape[0]
    head_count = decay_codes.shape[0]
    head_width = head_inputs.shape[1] // head_count
    state_width = input_proj.shape[1]
    increment_length = step_table(decay_codes)
    logarithm_decay = (
        -head_decay_speeds[:, None] * increment_length
        - sudden_falloff * boundary.astype(jnp.float32)[None, :]
    )
    cumul = jnp.cumsum(logarithm_decay, axis=1)
    group_total = cumul[:, -1]
    to_end = spread_heads(jnp.exp(group_total[:, None] - cumul), head_width)
    from_start = spread_heads(jnp.exp(cumul), head_width)
    scaled_in = head_inputs * spread_heads(increment_length, head_width)
    weighted_in = scaled_in * to_end
    weighted_grad = out_grad * from_start
    ends = jnp.einsum("tk,tn->kn", weighted_in, input_proj, precision=highest)
    starts = jnp.einsum("tk,tn->kn", weighted_grad, output_mapping, precision=highest)
    state_in, state_grad = chip_scans(
        ends.reshape(head_count, head_width, state_width),
        starts.reshape(head_count, head_width, state_width),
        group_total,
    )

    grad_scaled, grad_scores_t = block_terms(cumul, input_proj, output_mapping, scaled_in, out_grad)
    block_b = jnp.dot(grad_scores_t, output_mapping, precision=highest)
    block_c = jnp.einsum("st,sn->tn", grad_scores_t, input_proj, precision=highest)

    flat_in = state_in.reshape(head_count * head_width, state_width)
    flat_grad = state_grad.reshape(head_count * head_width, state_width)
    carry_c = jnp.dot(weighted_grad, flat_in, precision=highest)
    carry_b = jnp.dot(weighted_in, flat_grad, precision=highest)
    carry_x = to_end * jnp.einsum("tn,kn->tk", input_proj, flat_grad, precision=highest)
    grad_inputs = (grad_scaled + carry_x) * spread_heads(increment_length, head_width)

    both = jnp.concatenate([block_b + carry_b, block_c + carry_c], axis=1)
    parts = lax.axis_size("head")
    spread = lax.all_to_all(both, "head", 0, 0, tiled=True)
    summed = spread.reshape(parts, tok_count // parts, 2 * state_width).sum(axis=0)
    return (grad_inputs, summed[:, :state_width], summed[:, state_width:])


def solution(mesh):
    seq_count, head_parts = mesh.devices.shape
    split = jax.sharding.Mesh(
        mesh.devices.reshape(seq_count // 2, 2, head_parts), ("z", "core", "head")
    )
    seq = ("z", "core")
    return jax.shard_map(
        per_device,
        mesh=split,
        in_specs=(
            P(seq, "head"),
            P(seq, None),
            P(seq, None),
            P("head", seq),
            P(seq),
            P("head"),
            P(seq, "head"),
        ),
        out_specs=(P(seq, "head"), P(("z", "core", "head"), None), P(("z", "core", "head"), None)),
        check_vma=False,
    )
```

```python
import jax
import jax.numpy as jnp
from jax import lax
from jax.experimental import pallas as pl
from jax.experimental.pallas import tpu as pltpu
from jax.sharding import PartitionSpec as P

sudden_falloff = 0.35
highest = lax.Precision.HIGHEST
HEADS_PER_STEP = 4


def step_table(decay_codes):
    levels = jnp.arange(16, dtype=jnp.int32)
    values = 0.5 * 4.0 ** (levels.astype(jnp.float32) / 15.0)
    matching_label = decay_codes[None, :, :] == levels[:, None, None]
    return jnp.sum(jnp.where(matching_label, values[:, None, None], 0.0), axis=0)


def spread_heads(per_head, head_width):
    head_count, tok_count = per_head.shape
    wide = jnp.broadcast_to(per_head.T[:, :, None], (tok_count, head_count, head_width))
    return wide.reshape(tok_count, head_count * head_width)


def block_kernel(cum_ref, cum_t_ref, proj_in_ref, proj_out_ref, in_ref, grad_ref, flow_ref, acc_ref,
                 scores_t_ref):
    step = pl.program_id(0)

    @pl.when(step == 0)
    def _():
        acc_ref[...] = jnp.zeros_like(acc_ref)
        scores_t_ref[...] = lax.dot_general(
            proj_in_ref[...], proj_out_ref[...], (((1,), (1,)), ((), ())), precision=highest,
            preferred_element_type=jnp.float32,
        )

    tok = scores_t_ref.shape[0]
    width = in_ref.shape[1] // HEADS_PER_STEP
    head_count = cum_ref.shape[0]
    piece = 64
    which = lax.broadcasted_iota(jnp.int32, (tok, head_count), 1)
    for k in range(HEADS_PER_STEP):
        head = step * HEADS_PER_STEP + k
        cum_row = cum_ref[pl.ds(head, 1), :]
        cum_col = jnp.sum(jnp.where(which == head, cum_t_ref[...], 0.0), axis=1, keepdims=True)
        lanes = slice(k * width, (k + 1) * width)
        for first in range(0, tok, piece):
            span = tok - first
            rows = lax.broadcasted_iota(jnp.int32, (piece, span), 0)
            cols = lax.broadcasted_iota(jnp.int32, (piece, span), 1)
            later = cols >= rows
            gap = cum_row[:, first:] - cum_col[first:first + piece, :]
            decay_t = jnp.where(later, jnp.exp(gap), 0.0)
            own_in = in_ref[first:first + piece, lanes]
            own_grad = grad_ref[first:, lanes]
            flow_ref[first:first + piece, lanes] = jnp.dot(
                scores_t_ref[first:first + piece, first:] * decay_t, own_grad,
                precision=highest, preferred_element_type=jnp.float32,
            )
            pair_t = lax.dot_general(
                own_in, own_grad, (((1,), (1,)), ((), ())), precision=highest,
                preferred_element_type=jnp.float32,
            )
            acc_ref[first:first + piece, first:] += pair_t * decay_t


def block_terms(cumul, input_proj, output_mapping, scaled_in, out_grad):
    head_count, tok = cumul.shape
    chan = scaled_in.shape[1]
    state_width = input_proj.shape[1]
    lanes = chan // head_count * HEADS_PER_STEP
    return pl.pallas_call(
        block_kernel,
        grid=(head_count // HEADS_PER_STEP,),
        in_specs=[
            pl.BlockSpec((head_count, tok), lambda j: (0, 0)),
            pl.BlockSpec((tok, head_count), lambda j: (0, 0)),
            pl.BlockSpec((tok, state_width), lambda j: (0, 0)),
            pl.BlockSpec((tok, state_width), lambda j: (0, 0)),
            pl.BlockSpec((tok, lanes), lambda j: (0, j)),
            pl.BlockSpec((tok, lanes), lambda j: (0, j)),
        ],
        out_specs=[
            pl.BlockSpec((tok, lanes), lambda j: (0, j)),
            pl.BlockSpec((tok, tok), lambda j: (0, 0)),
        ],
        out_shape=[
            jax.ShapeDtypeStruct((tok, chan), jnp.float32),
            jax.ShapeDtypeStruct((tok, tok), jnp.float32),
        ],
        scratch_shapes=[pltpu.VMEM((tok, tok), jnp.float32)],
    )(cumul, cumul.T, input_proj, output_mapping, scaled_in, out_grad)


def pack_total(total, state_width):
    head_count = total.shape[0]
    rows = jnp.zeros((8, state_width), jnp.float32)
    return lax.dynamic_update_slice(
        rows, jnp.broadcast_to(total[:, None], (head_count, state_width)), (0, 0)
    )


def join(earlier, later, later_total):
    return jnp.exp(later_total)[:, None, None] * earlier + later


def pick(flag, when_true, when_false):
    return jnp.where(flag, when_true, when_false)


def chip_scans(ends, starts, total):
    chips = lax.axis_size("z")
    core = lax.axis_index("core")
    head_count, width, state_width = ends.shape
    rows = head_count * width
    both = ("z", "core")
    swap = [(0, 1), (1, 0)]
    is_fwd = core == 0
    mine = pick(is_fwd, ends, starts)
    other = pick(is_fwd, starts, ends)

    def packed(state, tot):
        return jnp.concatenate(
            [state.reshape(rows, state_width), pack_total(tot, state_width)], axis=0
        )

    def unpacked(value):
        return value[:rows].reshape(head_count, width, state_width), value[rows:rows + head_count, 0]

    def move(value, hop):
        pairs = []
        for z in range(chips):
            if z + hop < chips:
                pairs.append((2 * z, 2 * (z + hop)))
            if z - hop >= 0:
                pairs.append((2 * z + 1, 2 * (z - hop) + 1))
        return lax.ppermute(value, both, pairs)

    cross = []
    for z in range(chips):
        if z + 1 < chips:
            cross.append((2 * z + 1, 2 * (z + 1)))
        if z - 1 >= 0:
            cross.append((2 * z, 2 * (z - 1) + 1))
    near_state, near_t = unpacked(move(packed(mine, total), 1))
    far_state, far_t = unpacked(lax.ppermute(packed(other, total), both, cross))
    running = packed(join(near_state, far_state, far_t), near_t + far_t)
    hop = 1
    while hop < chips:
        got = move(running, hop)
        run_t = running[rows:rows + head_count, 0]
        scale = jnp.concatenate(
            [jnp.repeat(jnp.exp(run_t), width), jnp.ones((running.shape[0] - rows,), jnp.float32)]
        )
        running = scale[:, None] * got + running
        hop *= 2
    prefix, unused = unpacked(running)
    joined = join(prefix, mine, total)
    back = lax.ppermute(joined.reshape(rows, state_width), "core", swap)
    other = back.reshape(head_count, width, state_width)
    state_in = pick(is_fwd, prefix, other)
    state_grad = pick(is_fwd, other, prefix)
    return state_in, state_grad


def per_device(
    head_inputs, input_proj, output_mapping, decay_codes, boundary, head_decay_speeds, out_grad
):
    tok_count = head_inputs.shape[0]
    head_count = decay_codes.shape[0]
    head_width = head_inputs.shape[1] // head_count
    state_width = input_proj.shape[1]
    increment_length = step_table(decay_codes)
    logarithm_decay = (
        -head_decay_speeds[:, None] * increment_length
        - sudden_falloff * boundary.astype(jnp.float32)[None, :]
    )
    cumul = jnp.cumsum(logarithm_decay, axis=1)
    group_total = cumul[:, -1]
    to_end = spread_heads(jnp.exp(group_total[:, None] - cumul), head_width)
    from_start = spread_heads(jnp.exp(cumul), head_width)
    scaled_in = head_inputs * spread_heads(increment_length, head_width)
    weighted_in = scaled_in * to_end
    weighted_grad = out_grad * from_start
    ends = jnp.einsum("tk,tn->kn", weighted_in, input_proj, precision=highest)
    starts = jnp.einsum("tk,tn->kn", weighted_grad, output_mapping, precision=highest)
    state_in, state_grad = chip_scans(
        ends.reshape(head_count, head_width, state_width),
        starts.reshape(head_count, head_width, state_width),
        group_total,
    )

    grad_scaled, grad_scores_t = block_terms(cumul, input_proj, output_mapping, scaled_in, out_grad)
    block_b = jnp.dot(grad_scores_t, output_mapping, precision=highest)
    block_c = jnp.einsum("st,sn->tn", grad_scores_t, input_proj, precision=highest)

    flat_in = state_in.reshape(head_count * head_width, state_width)
    flat_grad = state_grad.reshape(head_count * head_width, state_width)
    carry_c = jnp.dot(weighted_grad, flat_in, precision=highest)
    carry_b = jnp.dot(weighted_in, flat_grad, precision=highest)
    carry_x = to_end * jnp.einsum("tn,kn->tk", input_proj, flat_grad, precision=highest)
    grad_inputs = (grad_scaled + carry_x) * spread_heads(increment_length, head_width)

    both = jnp.concatenate([block_b + carry_b, block_c + carry_c], axis=1)
    parts = lax.axis_size("head")
    spread = lax.all_to_all(both, "head", 0, 0, tiled=True)
    summed = spread.reshape(parts, tok_count // parts, 2 * state_width).sum(axis=0)
    return (grad_inputs, summed[:, :state_width], summed[:, state_width:])


def solution(mesh):
    seq_count, head_parts = mesh.devices.shape
    split = jax.sharding.Mesh(
        mesh.devices.reshape(seq_count // 2, 2, head_parts), ("z", "core", "head")
    )
    seq = ("z", "core")
    return jax.shard_map(
        per_device,
        mesh=split,
        in_specs=(
            P(seq, "head"),
            P(seq, None),
            P(seq, None),
            P("head", seq),
            P(seq),
            P("head"),
            P(seq, "head"),
        ),
        out_specs=(P(seq, "head"), P(("z", "core", "head"), None), P(("z", "core", "head"), None)),
        check_vma=False,
    )
```
